128 devices in a mesh: row: 4 (over z), col: 32 (over x, y, core).
Axes of the slice: x: 4, y: 4, z: 4, core: 2. Of those that a mesh axis runs over, the one named last changes fastest.
Arguments:
- matrix_real: bfloat16 [512, 16384], P('col', 'row'), may hold values from -0.25 to 0.25
- matrix_imag: bfloat16 [512, 16384], P('col', 'row'), may hold values from -0.25 to 0.25
- valence_index: int32 [512], P('col'), may hold values from 0 to 15
- conduction_index: int32 [512], P('col'), may hold values from 0 to 31
- valence_energy: float32 [16], replicated, may hold values from -1.5 to -0.1
- conduction_energy: float32 [32], replicated, may hold values from 0.1 to 2
- frequency: float32 [2], replicated, may hold values from 0.2 to 2
Outputs:
- chi_real: bfloat16 [2, 16384, 16384], P(None, 'row', 'col')
- chi_imag: bfloat16 [2, 16384, 16384], P(None, 'row', 'col')
The draws below stay inside these ranges and needn't reach their ends.
All inputs are finite; a program needn't handle non-finite values.
Results may differ from the reference program's by a relative error of at most 0.005.
Values may be sent and summed in bfloat16 or wider, within the bound.
No kernel may reach another device: no remote copies, remote signals or barrier semaphores. Data moves between devices by JAX's collectives and lax.ppermute only.
A program may use at most 192 MiB of HBM per device.

```python
import math
import jax
import jax.numpy as jnp

NG = 16384
NF = 2
NV = 16
NC = 32
NP = 512


def place_ends(entries, own_key, least, high):
    dims = entries.shape
    place = [jax.random.randint(jax.random.fold_in(own_key, axis), (), 0, dims[axis]) for axis in range(len(dims))]
    entries = entries.at[tuple(place)].set(least)
    longest = dims.index(max(dims))
    place[longest] = (place[longest] + 1) % dims[longest]
    return entries.at[tuple(place)].set(high)


def block_scale(stream_key, shape, split, low, high):
    loudness, own = 1.0, jax.random.fold_in(stream_key, 6)
    for position, blocks in split:
        steps = jnp.exp(jax.random.uniform(jax.random.fold_in(own, position), (blocks,), jnp.float32, low / len(split), high / len(split)))
        loudness = loudness * jnp.repeat(steps, shape[position] // blocks).reshape([-1 if axis == position else 1 for axis in range(len(shape))])
    return loudness


def gaussian(rng, extent, width, reach, pieces=(), dtype=jnp.bfloat16):
    array = jax.random.normal(rng, extent, jnp.float32) * width
    if len(pieces) > 0:
        array = block_scale(rng, extent, pieces, -0.22, 0.18) * array
    return jnp.clip(array, min=-reach, max=reach).astype(dtype)


def setup_inputs(seed: int = 0) -> dict:
    arg_keys = jax.random.split(jax.random.key(seed), 8)
    matrix_real = gaussian(arg_keys[0], (NP, NG), NP ** -0.5, 0.25, ((0, 32), (1, 4)))
    matrix_imag = gaussian(arg_keys[1], (NP, NG), NP ** -0.5, 0.25, ((0, 32), (1, 4)))
    valence_index = place_ends(jax.random.randint(arg_keys[2], (NP,), 0, NV), jax.random.fold_in(arg_keys[2], 1), 0, NV - 1).astype(jnp.int32)
    conduction_index = place_ends(jax.random.randint(arg_keys[3], (NP,), 0, NC), jax.random.fold_in(arg_keys[3], 1), 0, NC - 1).astype(jnp.int32)
    valence_energy = jnp.clip(jax.random.uniform(arg_keys[4], (NV,), jnp.float32, -1.5, -0.1), -1.5, -0.1)
    conduction_energy = jnp.clip(jax.random.uniform(arg_keys[5], (NC,), jnp.float32, 0.1, 2.0), 0.1, 2.0)
    frequency = jnp.clip(jnp.exp(jax.random.uniform(arg_keys[6], (NF,), jnp.float32, math.log(0.2), math.log(2.0))), 0.2, 2.0)
    return {"matrix_real": matrix_real, "matrix_imag": matrix_imag, "valence_index": valence_index, "conduction_index": conduction_index, "valence_energy": valence_energy, "conduction_energy": conduction_energy, "frequency": frequency}


def reference(matrix_real, matrix_imag, valence_index, conduction_index, valence_energy, conduction_energy, frequency):
    gap = conduction_energy[conduction_index] - valence_energy[valence_index]
    real_out = []
    imag_out = []
    for index in range(NF):
        omega = frequency[index]
        weight = 4.0 * gap / (gap * gap + omega * omega)
        scaled_real = (weight[:, None] * matrix_real.astype(jnp.float32)).astype(jnp.bfloat16)
        scaled_imag = (weight[:, None] * matrix_imag.astype(jnp.float32)).astype(jnp.bfloat16)
        chi_real = jnp.dot(matrix_real.T, scaled_real, preferred_element_type=jnp.float32)
        chi_real = -(chi_real + jnp.dot(matrix_imag.T, scaled_imag, preferred_element_type=jnp.float32))
        chi_imag = jnp.dot(matrix_real.T, scaled_imag, preferred_element_type=jnp.float32)
        chi_imag = -(chi_imag - jnp.dot(matrix_imag.T, scaled_real, preferred_element_type=jnp.float32))
        real_out.append(chi_real.astype(jnp.bfloat16))
        imag_out.append(chi_imag.astype(jnp.bfloat16))
    return jnp.stack(real_out, axis=0), jnp.stack(imag_out, axis=0)
```

```python
import jax
import jax.numpy as jnp
from jax import lax
from jax.sharding import PartitionSpec as P


def lookup(indices, table):
    count = table.shape[0]
    picks = indices[:, None] == lax.broadcasted_iota(jnp.int32, (1, count), 1)
    return jnp.sum(jnp.where(picks, table[None, :], 0.0), axis=1)


def contract(left_side, right_side):
    return lax.dot_general(
        left_side, right_side, (((0,), (0,)), ((), ())), preferred_element_type=jnp.float32
    )


CHUNKS = 4


def on_device(
    matrix_real,
    matrix_imag,
    valence_index,
    conduction_index,
    valence_energy,
    conduction_energy,
    frequency,
):
    ncol = lax.psum(1, "col")
    local_pairs, local_g = matrix_real.shape
    pairs = local_pairs * ncol
    both = jnp.stack([matrix_real, matrix_imag])
    bands = jnp.stack([valence_index, conduction_index]).astype(jnp.float32)
    all_bands = lax.all_gather(bands, "col", axis=1, tiled=True).astype(jnp.int32)
    gap = lookup(all_bands[1], conduction_energy) - lookup(all_bands[0], valence_energy)
    spread = lax.all_gather(both, "row", axis=2, tiled=True)
    spread = spread.reshape(2, local_pairs, ncol, -1)
    column = lax.all_to_all(spread, "col", split_axis=2, concat_axis=1, tiled=True)
    width = column.shape[-1]
    wide = column.reshape(2, pairs, width).astype(jnp.float32)
    right_real = []
    right_imag = []
    for index in range(frequency.shape[0]):
        omega = frequency[index]
        weight = 4.0 * gap / (gap * gap + omega * omega)
        scaled_real = (weight[:, None] * wide[0]).astype(jnp.bfloat16)
        scaled_imag = (weight[:, None] * wide[1]).astype(jnp.bfloat16)
        right_real.append(jnp.concatenate([-scaled_real, -scaled_imag], axis=0))
        right_imag.append(jnp.concatenate([-scaled_imag, scaled_real], axis=0))
    step = local_g // CHUNKS
    real_parts = [[] for _ in right_real]
    imag_parts = [[] for _ in right_real]
    for chunk in range(CHUNKS):
        piece = both[:, :, chunk * step : (chunk + 1) * step]
        left = lax.all_gather(piece, "col", axis=1, tiled=True).reshape(2 * pairs, step)
        for index in range(len(right_real)):
            real_parts[index].append(contract(left, right_real[index]).astype(jnp.bfloat16))
            imag_parts[index].append(contract(left, right_imag[index]).astype(jnp.bfloat16))
    chi_real = jnp.stack([jnp.concatenate(p, axis=0) for p in real_parts])
    chi_imag = jnp.stack([jnp.concatenate(p, axis=0) for p in imag_parts])
    return chi_real, chi_imag


def solution(mesh):
    placed = (P("col", "row"), P("col", "row"), P("col"), P("col"), P(), P(), P())
    return jax.shard_map(
        on_device,
        mesh=mesh,
        in_specs=placed,
        out_specs=(P(None, "row", "col"), P(None, "row", "col")),
        check_vma=False,
    )
```

```python
import jax
import jax.numpy as jnp
from jax import lax
from jax.sharding import PartitionSpec as P


def lookup(indices, table):
    count = table.shape[0]
    picks = indices[:, None] == lax.broadcasted_iota(jnp.int32, (1, count), 1)
    return jnp.sum(jnp.where(picks, table[None, :], 0.0), axis=1)


def on_device(
    matrix_real,
    matrix_imag,
    valence_index,
    conduction_index,
    valence_energy,
    conduction_energy,
    frequency,
):
    nrow = lax.psum(1, "row")
    ncol = lax.psum(1, "col")
    local_pairs, local_g = matrix_real.shape
    pairs = local_pairs * ncol
    width = local_g * nrow // ncol
    both = jnp.stack([matrix_real, matrix_imag])
    left = lax.all_gather(both, "col", axis=1, tiled=True).reshape(2 * pairs, local_g)
    copies = jnp.broadcast_to(both[None], (nrow,) + both.shape)
    spread = lax.all_to_all(copies, "row", 0, 0, tiled=True)
    spread = spread.reshape(nrow, 2, local_pairs, local_g // width, width)
    payload = spread.transpose(1, 2, 0, 3, 4).reshape(2, local_pairs, ncol, width)
    bands = jnp.stack([valence_index, conduction_index]).astype(jnp.bfloat16)
    tags = jnp.broadcast_to(bands[:, :, None, None], (2, local_pairs, ncol, 128))
    payload = jnp.concatenate([payload, tags], axis=3)
    column = lax.all_to_all(payload, "col", split_axis=2, concat_axis=1, tiled=True)
    column = column.reshape(2, pairs, width + 128)
    all_bands = column[:, :, width].astype(jnp.int32)
    gap = lookup(all_bands[1], conduction_energy) - lookup(all_bands[0], valence_energy)
    wide = column[:, :, :width].astype(jnp.float32)
    right_real = []
    right_imag = []
    for index in range(frequency.shape[0]):
        omega = frequency[index]
        weight = 4.0 * gap / (gap * gap + omega * omega)
        scaled_real = (weight[:, None] * wide[0]).astype(jnp.bfloat16)
        scaled_imag = (weight[:, None] * wide[1]).astype(jnp.bfloat16)
        right_real.append(jnp.concatenate([-scaled_real, -scaled_imag], axis=0))
        right_imag.append(jnp.concatenate([-scaled_imag, scaled_real], axis=0))
    nf = len(right_real)
    lefts = jnp.broadcast_to(left[None], (nf,) + left.shape)
    dims = (((1,), (1,)), ((0,), (0,)))
    chi_real = lax.dot_general(lefts, jnp.stack(right_real), dims, preferred_element_type=jnp.float32)
    chi_imag = lax.dot_general(lefts, jnp.stack(right_imag), dims, preferred_element_type=jnp.float32)
    return chi_real.astype(jnp.bfloat16), chi_imag.astype(jnp.bfloat16)


def solution(mesh):
    placed = (P("col", "row"), P("col", "row"), P("col"), P("col"), P(), P(), P())
    return jax.shard_map(
        on_device,
        mesh=mesh,
        in_specs=placed,
        out_specs=(P(None, "row", "col"), P(None, "row", "col")),
        check_vma=False,
    )
```

```python
import jax
import jax.numpy as jnp
from jax import lax
from jax.sharding import PartitionSpec as P


def lookup(indices, table):
    count = table.shape[0]
    picks = indices[:, None] == lax.broadcasted_iota(jnp.int32, (1, count), 1)
    return jnp.sum(jnp.where(picks, table[None, :], 0.0), axis=1)


def on_device(
    matrix_real,
    matrix_imag,
    valence_index,
    conduction_index,
    valence_energy,
    conduction_energy,
    frequency,
):
    nrow = lax.psum(1, "row")
    ncol = lax.psum(1, "col")
    local_pairs, local_g = matrix_real.shape
    pairs = local_pairs * ncol
    width = local_g * nrow // ncol
    both = jnp.stack([matrix_real, matrix_imag])
    left = lax.all_gather(both, "col", axis=1, tiled=True).reshape(2 * pairs, local_g)
    copies = jnp.broadcast_to(both[None], (nrow,) + both.shape)
    spread = lax.all_to_all(copies, "row", 0, 0, tiled=True)
    spread = spread.reshape(nrow, 2, local_pairs, local_g // width, width)
    payload = spread.transpose(1, 2, 0, 3, 4).reshape(2, local_pairs, ncol, width)
    bands = jnp.stack([valence_index, conduction_index]).astype(jnp.bfloat16)
    tags = jnp.broadcast_to(bands[:, :, None, None], (2, local_pairs, ncol, 128))
    payload = jnp.concatenate([payload, tags], axis=3)
    column = lax.all_to_all(payload, "col", split_axis=2, concat_axis=1, tiled=True)
    column = column.reshape(2, pairs, width + 128)
    all_bands = column[:, :, width].astype(jnp.int32)
    gap = lookup(all_bands[1], conduction_energy) - lookup(all_bands[0], valence_energy)
    wide = column[:, :, :width].astype(jnp.float32)
    right_real = []
    right_imag = []
    for index in range(frequency.shape[0]):
        omega = frequency[index]
        weight = 4.0 * gap / (gap * gap + omega * omega)
        scaled_real = (weight[:, None] * wide[0]).astype(jnp.bfloat16)
        scaled_imag = (weight[:, None] * wide[1]).astype(jnp.bfloat16)
        right_real.append(jnp.concatenate([-scaled_real, -scaled_imag], axis=0))
        right_imag.append(jnp.concatenate([-scaled_imag, scaled_real], axis=0))
    dims = (((0,), (0,)), ((), ()))
    chi_real = lax.dot_general(left, jnp.stack(right_real, axis=1), dims, preferred_element_type=jnp.float32)
    chi_imag = lax.dot_general(left, jnp.stack(right_imag, axis=1), dims, preferred_element_type=jnp.float32)
    chi_real = chi_real.transpose(1, 0, 2)
    chi_imag = chi_imag.transpose(1, 0, 2)
    return chi_real.astype(jnp.bfloat16), chi_imag.astype(jnp.bfloat16)


def solution(mesh):
    placed = (P("col", "row"), P("col", "row"), P("col"), P("col"), P(), P(), P())
    return jax.shard_map(
        on_device,
        mesh=mesh,
        in_specs=placed,
        out_specs=(P(None, "row", "col"), P(None, "row", "col")),
        check_vma=False,
    )
```

```python
import jax
import jax.numpy as jnp
from jax import lax
from jax.sharding import Mesh, PartitionSpec as P

CORE_PAIRS = [(0, 1), (1, 0)]


def lookup(indices, table):
    count = table.shape[0]
    picks = indices[:, None] == lax.broadcasted_iota(jnp.int32, (1, count), 1)
    return jnp.sum(jnp.where(picks, table[None, :], 0.0), axis=1)


def shift(value, axis, step):
    size = lax.psum(1, axis)
    return lax.ppermute(value, axis, [(i, (i + step) % size) for i in range(size)])


def ring_gather(block, axis):
    half = block.shape[-1] // 2
    from_minus = shift(block, axis, 1)
    from_plus = shift(block, axis, -1)
    far_first = shift(from_minus[..., :half], axis, 1)
    far_second = shift(from_plus[..., half:], axis, -1)
    far = jnp.concatenate([far_first, far_second], axis=-1)
    return jnp.stack([block, from_plus, far, from_minus])


def on_device(
    matrix_real,
    matrix_imag,
    valence_index,
    conduction_index,
    valence_energy,
    conduction_energy,
    frequency,
):
    cols = ("x", "y", "core")
    nrow = lax.psum(1, "row")
    nx, ny, ncore = lax.psum(1, "x"), lax.psum(1, "y"), lax.psum(1, "core")
    ncol = nx * ny * ncore
    local_pairs, local_g = matrix_real.shape
    pairs = local_pairs * ncol
    width = local_g * nrow // ncol
    both = jnp.stack([matrix_real, matrix_imag])

    row_real = ring_gather(matrix_real, "x")
    col_imag = ring_gather(matrix_imag, "y")
    all_real = ring_gather(row_real, "y")
    all_imag = ring_gather(col_imag, "x")
    mine = jnp.stack([all_real, all_imag.transpose(1, 0, 2, 3)])
    other = lax.ppermute(mine, "core", CORE_PAIRS)
    left = jnp.stack([mine, other], axis=3)
    left = left.transpose(0, 2, 1, 3, 4, 5).reshape(2 * pairs, local_g)

    copies = jnp.broadcast_to(both[None], (nrow,) + both.shape)
    spread = lax.all_to_all(copies, "row", 0, 0, tiled=True)
    spread = spread.reshape(nrow, 2, local_pairs, local_g // width, width)
    payload = spread.transpose(1, 2, 0, 3, 4).reshape(2, local_pairs, ncol, width)
    bands = jnp.stack([valence_index, conduction_index]).astype(jnp.bfloat16)
    tags = jnp.broadcast_to(bands[:, :, None, None], (2, local_pairs, ncol, 128))
    payload = jnp.concatenate([payload, tags], axis=3)
    column = lax.all_to_all(payload, cols, split_axis=2, concat_axis=1, tiled=True)
    column = column.reshape(2, pairs, width + 128)
    all_bands = column[:, :, width].astype(jnp.int32)
    gap = lookup(all_bands[1], conduction_energy) - lookup(all_bands[0], valence_energy)
    wide = column[:, :, :width].astype(jnp.float32)
    here = (lax.axis_index("x"), lax.axis_index("y"), lax.axis_index("core"))

    def relative(scaled):
        grid = scaled.reshape(nx, ny, ncore, local_pairs, width)
        for axis, start in enumerate(here):
            size = grid.shape[axis]
            doubled = jnp.concatenate([grid, grid], axis=axis)
            grid = lax.dynamic_slice_in_dim(doubled, start, size, axis=axis)
        return grid.reshape(pairs, width)

    right_real = []
    right_imag = []
    for index in range(frequency.shape[0]):
        omega = frequency[index]
        weight = 4.0 * gap / (gap * gap + omega * omega)
        scaled_real = relative((weight[:, None] * wide[0]).astype(jnp.bfloat16))
        scaled_imag = relative((weight[:, None] * wide[1]).astype(jnp.bfloat16))
        right_real.append(jnp.concatenate([-scaled_real, -scaled_imag], axis=0))
        right_imag.append(jnp.concatenate([-scaled_imag, scaled_real], axis=0))
    dims = (((0,), (0,)), ((), ()))
    chi_real = lax.dot_general(left, jnp.stack(right_real, axis=1), dims, preferred_element_type=jnp.float32)
    chi_imag = lax.dot_general(left, jnp.stack(right_imag, axis=1), dims, preferred_element_type=jnp.float32)
    chi_real = chi_real.transpose(1, 0, 2)
    chi_imag = chi_imag.transpose(1, 0, 2)
    return chi_real.astype(jnp.bfloat16), chi_imag.astype(jnp.bfloat16)


def solution(mesh):
    rows, cols = mesh.devices.shape
    grid = Mesh(mesh.devices.reshape(rows, 4, cols // 8, 2), ("row", "x", "y", "core"))
    cols = ("x", "y", "core")
    placed = (P(cols, "row"), P(cols, "row"), P(cols), P(cols), P(), P(), P())
    return jax.shard_map(
        on_device,
        mesh=grid,
        in_specs=placed,
        out_specs=(P(None, "row", cols), P(None, "row", cols)),
        check_vma=False,
    )
```

```python
import jax
import jax.numpy as jnp
from jax import lax
from jax.sharding import Mesh, PartitionSpec as P

CORE_PAIRS = [(0, 1), (1, 0)]


def lookup(indices, table):
    count = table.shape[0]
    picks = indices[:, None] == lax.broadcasted_iota(jnp.int32, (1, count), 1)
    return jnp.sum(jnp.where(picks, table[None, :], 0.0), axis=1)


def shift(value, axis, step):
    size = lax.psum(1, axis)
    return lax.ppermute(value, axis, [(i, (i + step) % size) for i in range(size)])


def ring_gather(block, axis):
    half = block.shape[-1] // 2
    from_minus = shift(block, axis, 1)
    from_plus = shift(block, axis, -1)
    far_first = shift(from_minus[..., :half], axis, 1)
    far_second = shift(from_plus[..., half:], axis, -1)
    far = jnp.concatenate([far_first, far_second], axis=-1)
    return from_plus, far, from_minus


def on_device(
    matrix_real,
    matrix_imag,
    valence_index,
    conduction_index,
    valence_energy,
    conduction_energy,
    frequency,
):
    cols = ("x", "y", "core")
    nrow = lax.psum(1, "row")
    nx, ny, ncore = lax.psum(1, "x"), lax.psum(1, "y"), lax.psum(1, "core")
    ncol = nx * ny * ncore
    local_pairs, local_g = matrix_real.shape
    pairs = local_pairs * ncol
    width = local_g * nrow // ncol
    both = jnp.stack([matrix_real, matrix_imag])

    row_real = jnp.stack((matrix_real,) + ring_gather(matrix_real, "x"))
    col_imag = jnp.stack((matrix_imag,) + ring_gather(matrix_imag, "y"))
    first = jnp.stack([row_real, col_imag])
    first_other = lax.ppermute(first, "core", CORE_PAIRS)
    real_plus, real_far, real_minus = ring_gather(row_real, "y")
    imag_plus, imag_far, imag_minus = ring_gather(col_imag, "x")
    near = jnp.stack([real_plus, real_minus, imag_plus, imag_minus])
    near_other = lax.ppermute(near, "core", CORE_PAIRS)
    far = jnp.stack([real_far, imag_far])
    far_other = lax.ppermute(far, "core", CORE_PAIRS)
    parts = []
    for part in range(2):
        for src_first, src_near, src_far in ((first, near, far), (first_other, near_other, far_other)):
            parts.append(
                jnp.stack([src_first[part], src_near[2 * part], src_far[part], src_near[2 * part + 1]])
            )
    left = jnp.stack(parts).reshape(2 * pairs, local_g)

    copies = jnp.broadcast_to(both[None], (nrow,) + both.shape)
    spread = lax.all_to_all(copies, "row", 0, 0, tiled=True)
    spread = spread.reshape(nrow, 2, local_pairs, local_g // width, width)
    payload = spread.transpose(1, 2, 0, 3, 4).reshape(2, local_pairs, ncol, width)
    bands = jnp.stack([valence_index, conduction_index]).astype(jnp.bfloat16)
    tags = jnp.broadcast_to(bands[:, :, None, None], (2, local_pairs, ncol, 128))
    payload = jnp.concatenate([payload, tags], axis=3)
    column = lax.all_to_all(payload, cols, split_axis=2, concat_axis=1, tiled=True)
    column = column.reshape(2, pairs, width + 128)
    all_bands = column[:, :, width].astype(jnp.int32)
    gap = lookup(all_bands[1], conduction_energy) - lookup(all_bands[0], valence_energy)
    wide = column[:, :, :width].astype(jnp.float32)
    here = (lax.axis_index("x"), lax.axis_index("y"), lax.axis_index("core"))

    def relative(scaled, order):
        grid = scaled.reshape(nx, ny, ncore, local_pairs, width)
        for axis, start in enumerate(here):
            size = grid.shape[axis]
            doubled = jnp.concatenate([grid, grid], axis=axis)
            grid = lax.dynamic_slice_in_dim(doubled, start, size, axis=axis)
        return grid.transpose(order + (3, 4)).reshape(pairs, width)

    real_order = (2, 1, 0)
    imag_order = (2, 0, 1)
    right_real = []
    right_imag = []
    for index in range(frequency.shape[0]):
        omega = frequency[index]
        weight = 4.0 * gap / (gap * gap + omega * omega)
        scaled_real = (weight[:, None] * wide[0]).astype(jnp.bfloat16)
        scaled_imag = (weight[:, None] * wide[1]).astype(jnp.bfloat16)
        real_a = relative(scaled_real, real_order)
        imag_b = relative(scaled_imag, imag_order)
        real_b = relative(scaled_real, imag_order)
        imag_a = relative(scaled_imag, real_order)
        right_real.append(jnp.concatenate([-real_a, -imag_b], axis=0))
        right_imag.append(jnp.concatenate([-imag_a, real_b], axis=0))
    dims = (((0,), (0,)), ((), ()))
    chi_real = lax.dot_general(left, jnp.stack(right_real, axis=1), dims, preferred_element_type=jnp.float32)
    chi_imag = lax.dot_general(left, jnp.stack(right_imag, axis=1), dims, preferred_element_type=jnp.float32)
    chi_real = chi_real.transpose(1, 0, 2)
    chi_imag = chi_imag.transpose(1, 0, 2)
    return chi_real.astype(jnp.bfloat16), chi_imag.astype(jnp.bfloat16)


def solution(mesh):
    rows, cols = mesh.devices.shape
    grid = Mesh(mesh.devices.reshape(rows, 4, cols // 8, 2), ("row", "x", "y", "core"))
    cols = ("x", "y", "core")
    placed = (P(cols, "row"), P(cols, "row"), P(cols), P(cols), P(), P(), P())
    return jax.shard_map(
        on_device,
        mesh=grid,
        in_specs=placed,
        out_specs=(P(None, "row", cols), P(None, "row", cols)),
        check_vma=False,
    )
```

```python
import jax
import jax.numpy as jnp
from jax import lax
from jax.sharding import Mesh, PartitionSpec as P

CORE_PAIRS = [(0, 1), (1, 0)]


def lookup(indices, table):
    count = table.shape[0]
    picks = indices[:, None] == lax.broadcasted_iota(jnp.int32, (1, count), 1)
    return jnp.sum(jnp.where(picks, table[None, :], 0.0), axis=1)


def shift(value, axis, step):
    size = lax.psum(1, axis)
    return lax.ppermute(value, axis, [(i, (i + step) % size) for i in range(size)])


def ring_gather(block, axis):
    half = block.shape[-1] // 2
    from_minus = shift(block, axis, 1)
    from_plus = shift(block, axis, -1)
    far_first = shift(from_minus[..., :half], axis, 1)
    far_second = shift(from_plus[..., half:], axis, -1)
    far = jnp.concatenate([far_first, far_second], axis=-1)
    return from_plus, far, from_minus


def on_device(
    matrix_real,
    matrix_imag,
    valence_index,
    conduction_index,
    valence_energy,
    conduction_energy,
    frequency,
):
    cols = ("x", "y", "core")
    nrow = lax.psum(1, "row")
    nx, ny, ncore = lax.psum(1, "x"), lax.psum(1, "y"), lax.psum(1, "core")
    ncol = nx * ny * ncore
    local_pairs, local_g = matrix_real.shape
    pairs = local_pairs * ncol
    width = local_g * nrow // ncol
    both = jnp.stack([matrix_real, matrix_imag])

    copies = jnp.broadcast_to(both[None], (nrow,) + both.shape)
    spread = lax.all_to_all(copies, "row", 0, 0, tiled=True)
    spread = spread.reshape(nrow, 2, local_pairs, local_g // width, width)
    row_real = jnp.stack((matrix_real,) + ring_gather(matrix_real, "x"))
    col_imag = jnp.stack((matrix_imag,) + ring_gather(matrix_imag, "y"))
    first = jnp.stack([row_real, col_imag])
    first_other = lax.ppermute(first, "core", CORE_PAIRS)
    spread, row_real, col_imag, first = lax.optimization_barrier((spread, row_real, col_imag, first))
    payload = spread.transpose(1, 2, 0, 3, 4).reshape(2, local_pairs, ncol, width)
    bands = jnp.stack([valence_index, conduction_index]).astype(jnp.bfloat16)
    tags = jnp.broadcast_to(bands[:, :, None, None], (2, local_pairs, ncol, 128))
    payload = jnp.concatenate([payload, tags], axis=3)
    column = lax.all_to_all(payload, cols, split_axis=2, concat_axis=1, tiled=True)
    column = column.reshape(2, pairs, width + 128)
    real_plus, real_far, real_minus = ring_gather(row_real, "y")
    imag_plus, imag_far, imag_minus = ring_gather(col_imag, "x")
    near = jnp.stack([real_plus, real_minus, imag_plus, imag_minus])
    near_other = lax.ppermute(near, "core", CORE_PAIRS)
    far = jnp.stack([real_far, imag_far])
    far_other = lax.ppermute(far, "core", CORE_PAIRS)
    parts = []
    for part in range(2):
        for src_first, src_near, src_far in ((first, near, far), (first_other, near_other, far_other)):
            parts.append(
                jnp.stack([src_first[part], src_near[2 * part], src_far[part], src_near[2 * part + 1]])
            )
    left = jnp.stack(parts).reshape(2 * pairs, local_g)

    all_bands = column[:, :, width].astype(jnp.int32)
    gap = lookup(all_bands[1], conduction_energy) - lookup(all_bands[0], valence_energy)
    wide = column[:, :, :width].astype(jnp.float32)
    here = (lax.axis_index("x"), lax.axis_index("y"), lax.axis_index("core"))

    def relative(scaled, order):
        grid = scaled.reshape(nx, ny, ncore, local_pairs, width)
        for axis, start in enumerate(here):
            size = grid.shape[axis]
            doubled = jnp.concatenate([grid, grid], axis=axis)
            grid = lax.dynamic_slice_in_dim(doubled, start, size, axis=axis)
        return grid.transpose(order + (3, 4)).reshape(pairs, width)

    real_order = (2, 1, 0)
    imag_order = (2, 0, 1)
    right_real = []
    right_imag = []
    for index in range(frequency.shape[0]):
        omega = frequency[index]
        weight = 4.0 * gap / (gap * gap + omega * omega)
        scaled_real = (weight[:, None] * wide[0]).astype(jnp.bfloat16)
        scaled_imag = (weight[:, None] * wide[1]).astype(jnp.bfloat16)
        real_a = relative(scaled_real, real_order)
        imag_b = relative(scaled_imag, imag_order)
        real_b = relative(scaled_real, imag_order)
        imag_a = relative(scaled_imag, real_order)
        right_real.append(jnp.concatenate([-real_a, -imag_b], axis=0))
        right_imag.append(jnp.concatenate([-imag_a, real_b], axis=0))
    dims = (((0,), (0,)), ((), ()))
    chi_real = lax.dot_general(left, jnp.stack(right_real, axis=1), dims, preferred_element_type=jnp.float32)
    chi_imag = lax.dot_general(left, jnp.stack(right_imag, axis=1), dims, preferred_element_type=jnp.float32)
    chi_real = chi_real.transpose(1, 0, 2)
    chi_imag = chi_imag.transpose(1, 0, 2)
    return chi_real.astype(jnp.bfloat16), chi_imag.astype(jnp.bfloat16)


def solution(mesh):
    rows, cols = mesh.devices.shape
    grid = Mesh(mesh.devices.reshape(rows, 4, cols // 8, 2), ("row", "x", "y", "core"))
    cols = ("x", "y", "core")
    placed = (P(cols, "row"), P(cols, "row"), P(cols), P(cols), P(), P(), P())
    return jax.shard_map(
        on_device,
        mesh=grid,
        in_specs=placed,
        out_specs=(P(None, "row", cols), P(None, "row", cols)),
        check_vma=False,
    )
```

```python
import jax
import jax.numpy as jnp
from jax import lax
from jax.sharding import Mesh, PartitionSpec as P

CORE_PAIRS = [(0, 1), (1, 0)]


def lookup(indices, table):
    count = table.shape[0]
    picks = indices[:, None] == lax.broadcasted_iota(jnp.int32, (1, count), 1)
    return jnp.sum(jnp.where(picks, table[None, :], 0.0), axis=1)


def shift(value, axis, step):
    size = lax.psum(1, axis)
    return lax.ppermute(value, axis, [(i, (i + step) % size) for i in range(size)])


def ring_gather(block, axis):
    half = block.shape[-1] // 2
    from_minus = shift(block, axis, 1)
    from_plus = shift(block, axis, -1)
    far_first = shift(from_minus[..., :half], axis, 1)
    far_second = shift(from_plus[..., half:], axis, -1)
    far = jnp.concatenate([far_first, far_second], axis=-1)
    return from_plus, far, from_minus


def on_device(
    matrix_real,
    matrix_imag,
    valence_index,
    conduction_index,
    valence_energy,
    conduction_energy,
    frequency,
):
    cols = ("x", "y", "core")
    nrow = lax.psum(1, "row")
    nx, ny, ncore = lax.psum(1, "x"), lax.psum(1, "y"), lax.psum(1, "core")
    ncol = nx * ny * ncore
    local_pairs, local_g = matrix_real.shape
    pairs = local_pairs * ncol
    width = local_g * nrow // ncol
    both = jnp.stack([matrix_real, matrix_imag])

    copies = jnp.broadcast_to(both[None], (nrow,) + both.shape)
    spread = lax.all_to_all(copies, "row", 0, 0, tiled=True)
    spread = spread.reshape(nrow, 2, local_pairs, local_g // width, width)
    row_real = jnp.stack((matrix_real,) + ring_gather(matrix_real, "x"))
    col_imag = jnp.stack((matrix_imag,) + ring_gather(matrix_imag, "y"))
    first = jnp.stack([row_real, col_imag])
    first_other = lax.ppermute(first, "core", CORE_PAIRS)
    spread, row_real, col_imag, first = lax.optimization_barrier((spread, row_real, col_imag, first))
    payload = spread.transpose(1, 2, 0, 3, 4).reshape(2, local_pairs, ncol, width)
    bands = jnp.stack([valence_index, conduction_index]).astype(jnp.bfloat16)
    tags = jnp.broadcast_to(bands[:, :, None, None], (2, local_pairs, ncol, 128))
    payload = jnp.concatenate([payload, tags], axis=3)
    column = lax.all_to_all(payload, cols, split_axis=2, concat_axis=1, tiled=True)
    column = column.reshape(2, pairs, width + 128)
    real_plus, real_far, real_minus = ring_gather(row_real, "y")
    imag_plus, imag_far, imag_minus = ring_gather(col_imag, "x")
    near = jnp.stack([real_plus, real_minus, imag_plus, imag_minus])
    near_other = lax.ppermute(near, "core", CORE_PAIRS)
    far = jnp.stack([real_far, imag_far])
    far_other = lax.ppermute(far, "core", CORE_PAIRS)
    halves = []
    for src_first, src_near, src_far in ((first, near, far), (first_other, near_other, far_other)):
        parts = []
        for part in range(2):
            parts.append(
                jnp.stack([src_first[part], src_near[2 * part], src_far[part], src_near[2 * part + 1]])
            )
        halves.append(jnp.stack(parts).reshape(pairs, local_g))

    all_bands = column[:, :, width].astype(jnp.int32)
    gap = lookup(all_bands[1], conduction_energy) - lookup(all_bands[0], valence_energy)
    wide = column[:, :, :width].astype(jnp.float32)
    here = (lax.axis_index("x"), lax.axis_index("y"), lax.axis_index("core"))

    def relative(scaled, order):
        grid = scaled.reshape(nx, ny, ncore, local_pairs, width)
        for axis, start in enumerate(here):
            size = grid.shape[axis]
            doubled = jnp.concatenate([grid, grid], axis=axis)
            grid = lax.dynamic_slice_in_dim(doubled, start, size, axis=axis)
        return grid.transpose(order + (3, 4)).reshape(pairs, width)

    real_order = (2, 1, 0)
    imag_order = (2, 0, 1)
    right_real = []
    right_imag = []
    for index in range(frequency.shape[0]):
        omega = frequency[index]
        weight = 4.0 * gap / (gap * gap + omega * omega)
        scaled_real = (weight[:, None] * wide[0]).astype(jnp.bfloat16)
        scaled_imag = (weight[:, None] * wide[1]).astype(jnp.bfloat16)
        real_a = relative(scaled_real, real_order)
        imag_b = relative(scaled_imag, imag_order)
        real_b = relative(scaled_real, imag_order)
        imag_a = relative(scaled_imag, real_order)
        right_real.append(jnp.stack([-real_a, -imag_b]))
        right_imag.append(jnp.stack([-imag_a, real_b]))
    dims = (((0,), (0,)), ((), ()))
    span = pairs // ncore
    outputs = []
    for right in (right_real, right_imag):
        right = jnp.stack(right, axis=2)
        total = None
        for core, half in enumerate(halves):
            piece = right[:, core * span : (core + 1) * span].reshape(pairs, frequency.shape[0], width)
            term = lax.dot_general(half, piece, dims, preferred_element_type=jnp.float32)
            total = term if total is None else total + term
        outputs.append(total.transpose(1, 0, 2).astype(jnp.bfloat16))
    return tuple(outputs)


def solution(mesh):
    rows, cols = mesh.devices.shape
    grid = Mesh(mesh.devices.reshape(rows, 4, cols // 8, 2), ("row", "x", "y", "core"))
    cols = ("x", "y", "core")
    placed = (P(cols, "row"), P(cols, "row"), P(cols), P(cols), P(), P(), P())
    return jax.shard_map(
        on_device,
        mesh=grid,
        in_specs=placed,
        out_specs=(P(None, "row", cols), P(None, "row", cols)),
        check_vma=False,
    )
```

```python
import jax
import jax.numpy as jnp
from jax import lax
from jax.sharding import Mesh, PartitionSpec as P

CORE_PAIRS = [(0, 1), (1, 0)]


def lookup(indices, table):
    count = table.shape[0]
    picks = indices[:, None] == lax.broadcasted_iota(jnp.int32, (1, count), 1)
    return jnp.sum(jnp.where(picks, table[None, :], 0.0), axis=1)


def shift(value, axis, step):
    size = lax.psum(1, axis)
    return lax.ppermute(value, axis, [(i, (i + step) % size) for i in range(size)])


def ring_gather(block, axis):
    return shift(block, axis, -1), shift(block, axis, 2), shift(block, axis, 1)


def on_device(
    matrix_real,
    matrix_imag,
    valence_index,
    conduction_index,
    valence_energy,
    conduction_energy,
    frequency,
):
    cols = ("x", "y", "core")
    nrow = lax.psum(1, "row")
    nx, ny, ncore = lax.psum(1, "x"), lax.psum(1, "y"), lax.psum(1, "core")
    ncol = nx * ny * ncore
    local_pairs, local_g = matrix_real.shape
    pairs = local_pairs * ncol
    width = local_g * nrow // ncol
    both = jnp.stack([matrix_real, matrix_imag])

    copies = jnp.broadcast_to(both[None], (nrow,) + both.shape)
    spread = lax.all_to_all(copies, "row", 0, 0, tiled=True)
    spread = spread.reshape(nrow, 2, local_pairs, local_g // width, width)
    row_real = jnp.stack((matrix_real,) + ring_gather(matrix_real, "x"))
    col_imag = jnp.stack((matrix_imag,) + ring_gather(matrix_imag, "y"))
    first = jnp.stack([row_real, col_imag])
    first_other = lax.ppermute(first, "core", CORE_PAIRS)
    spread, row_real, col_imag, first = lax.optimization_barrier((spread, row_real, col_imag, first))
    payload = spread.transpose(1, 2, 0, 3, 4).reshape(2, local_pairs, ncol, width)
    bands = jnp.stack([valence_index, conduction_index]).astype(jnp.bfloat16)
    tags = jnp.broadcast_to(bands[:, :, None, None], (2, local_pairs, ncol, 128))
    payload = jnp.concatenate([payload, tags], axis=3)
    column = lax.all_to_all(payload, cols, split_axis=2, concat_axis=1, tiled=True)
    column = column.reshape(2, pairs, width + 128)
    real_plus, real_far, real_minus = ring_gather(row_real, "y")
    imag_plus, imag_far, imag_minus = ring_gather(col_imag, "x")
    near = jnp.stack([real_plus, real_minus, imag_plus, imag_minus])
    near_other = lax.ppermute(near, "core", CORE_PAIRS)
    far = jnp.stack([real_far, imag_far])
    far_other = lax.ppermute(far, "core", CORE_PAIRS)
    parts = []
    for part in range(2):
        for src_first, src_near, src_far in ((first, near, far), (first_other, near_other, far_other)):
            parts.append(
                jnp.stack([src_first[part], src_near[2 * part], src_far[part], src_near[2 * part + 1]])
            )
    left = jnp.stack(parts).reshape(2 * pairs, local_g)

    all_bands = column[:, :, width].astype(jnp.int32)
    gap = lookup(all_bands[1], conduction_energy) - lookup(all_bands[0], valence_energy)
    wide = column[:, :, :width].astype(jnp.float32)
    here = (lax.axis_index("x"), lax.axis_index("y"), lax.axis_index("core"))

    def relative(scaled, order):
        grid = scaled.reshape(nx, ny, ncore, local_pairs, width)
        for axis, start in enumerate(here):
            size = grid.shape[axis]
            doubled = jnp.concatenate([grid, grid], axis=axis)
            grid = lax.dynamic_slice_in_dim(doubled, start, size, axis=axis)
        return grid.transpose(order + (3, 4)).reshape(pairs, width)

    real_order = (2, 1, 0)
    imag_order = (2, 0, 1)
    right_real = []
    right_imag = []
    for index in range(frequency.shape[0]):
        omega = frequency[index]
        weight = 4.0 * gap / (gap * gap + omega * omega)
        scaled_real = (weight[:, None] * wide[0]).astype(jnp.bfloat16)
        scaled_imag = (weight[:, None] * wide[1]).astype(jnp.bfloat16)
        real_a = relative(scaled_real, real_order)
        imag_b = relative(scaled_imag, imag_order)
        real_b = relative(scaled_real, imag_order)
        imag_a = relative(scaled_imag, real_order)
        right_real.append(jnp.concatenate([-real_a, -imag_b], axis=0))
        right_imag.append(jnp.concatenate([-imag_a, real_b], axis=0))
    dims = (((0,), (0,)), ((), ()))
    chi_real = lax.dot_general(left, jnp.stack(right_real, axis=1), dims, preferred_element_type=jnp.float32)
    chi_imag = lax.dot_general(left, jnp.stack(right_imag, axis=1), dims, preferred_element_type=jnp.float32)
    chi_real = chi_real.transpose(1, 0, 2)
    chi_imag = chi_imag.transpose(1, 0, 2)
    return chi_real.astype(jnp.bfloat16), chi_imag.astype(jnp.bfloat16)


def solution(mesh):
    rows, cols = mesh.devices.shape
    grid = Mesh(mesh.devices.reshape(rows, 4, cols // 8, 2), ("row", "x", "y", "core"))
    cols = ("x", "y", "core")
    placed = (P(cols, "row"), P(cols, "row"), P(cols), P(cols), P(), P(), P())
    return jax.shard_map(
        on_device,
        mesh=grid,
        in_specs=placed,
        out_specs=(P(None, "row", cols), P(None, "row", cols)),
        check_vma=False,
    )
```

```python
import jax
import jax.numpy as jnp
from jax import lax
from jax.sharding import Mesh, PartitionSpec as P

CORE_PAIRS = [(0, 1), (1, 0)]


def lookup(indices, table):
    count = table.shape[0]
    picks = indices[:, None] == lax.broadcasted_iota(jnp.int32, (1, count), 1)
    return jnp.sum(jnp.where(picks, table[None, :], 0.0), axis=1)


def shift(value, axis, step):
    size = lax.psum(1, axis)
    return lax.ppermute(value, axis, [(i, (i + step) % size) for i in range(size)])


def ring_gather(block, axis):
    half = block.shape[-1] // 2
    from_minus = shift(block, axis, 1)
    from_plus = shift(block, axis, -1)
    far_first = shift(from_minus[..., :half], axis, 1)
    far_second = shift(from_plus[..., half:], axis, -1)
    far = jnp.concatenate([far_first, far_second], axis=-1)
    return from_plus, far, from_minus


def on_device(
    matrix_real,
    matrix_imag,
    valence_index,
    conduction_index,
    valence_energy,
    conduction_energy,
    frequency,
):
    cols = ("x", "y", "core")
    nrow = lax.psum(1, "row")
    nx, ny, ncore = lax.psum(1, "x"), lax.psum(1, "y"), lax.psum(1, "core")
    ncol = nx * ny * ncore
    local_pairs, local_g = matrix_real.shape
    pairs = local_pairs * ncol
    width = local_g * nrow // ncol
    both = jnp.stack([matrix_real, matrix_imag])

    copies = jnp.broadcast_to(both[None], (nrow,) + both.shape)
    spread = lax.all_to_all(copies, "row", 0, 0, tiled=True)
    spread = spread.reshape(nrow, 2, local_pairs, local_g // width, width)
    left_imag = lax.all_gather(matrix_imag, cols, axis=0, tiled=True)
    row_real = jnp.stack((matrix_real,) + ring_gather(matrix_real, "x"))
    first_other = lax.ppermute(row_real, "core", CORE_PAIRS)
    spread, row_real = lax.optimization_barrier((spread, row_real))
    payload = spread.transpose(1, 2, 0, 3, 4).reshape(2, local_pairs, ncol, width)
    bands = jnp.stack([valence_index, conduction_index]).astype(jnp.bfloat16)
    tags = jnp.broadcast_to(bands[:, :, None, None], (2, local_pairs, ncol, 128))
    payload = jnp.concatenate([payload, tags], axis=3)
    column = lax.all_to_all(payload, cols, split_axis=2, concat_axis=1, tiled=True)
    column = column.reshape(2, pairs, width + 128)
    real_plus, real_far, real_minus = ring_gather(row_real, "y")
    near = jnp.stack([real_plus, real_minus])
    near_other = lax.ppermute(near, "core", CORE_PAIRS)
    far_other = lax.ppermute(real_far, "core", CORE_PAIRS)
    own = jnp.stack([row_real, real_plus, real_far, real_minus])
    other = jnp.stack([first_other, near_other[0], far_other, near_other[1]])
    left = jnp.concatenate([own.reshape(pairs // 2, local_g), other.reshape(pairs // 2, local_g), left_imag])

    all_bands = column[:, :, width].astype(jnp.int32)
    gap = lookup(all_bands[1], conduction_energy) - lookup(all_bands[0], valence_energy)
    wide = column[:, :, :width].astype(jnp.float32)
    here = (lax.axis_index("x"), lax.axis_index("y"), lax.axis_index("core"))

    def relative(scaled, order):
        grid = scaled.reshape(nx, ny, ncore, local_pairs, width)
        for axis, start in enumerate(here):
            size = grid.shape[axis]
            doubled = jnp.concatenate([grid, grid], axis=axis)
            grid = lax.dynamic_slice_in_dim(doubled, start, size, axis=axis)
        return grid.transpose(order + (3, 4)).reshape(pairs, width)

    real_order = (2, 1, 0)
    right_real = []
    right_imag = []
    for index in range(frequency.shape[0]):
        omega = frequency[index]
        weight = 4.0 * gap / (gap * gap + omega * omega)
        scaled_real = (weight[:, None] * wide[0]).astype(jnp.bfloat16)
        scaled_imag = (weight[:, None] * wide[1]).astype(jnp.bfloat16)
        real_a = relative(scaled_real, real_order)
        imag_a = relative(scaled_imag, real_order)
        right_real.append(jnp.concatenate([-real_a, -scaled_imag], axis=0))
        right_imag.append(jnp.concatenate([-imag_a, scaled_real], axis=0))
    dims = (((0,), (0,)), ((), ()))
    chi_real = lax.dot_general(left, jnp.stack(right_real, axis=1), dims, preferred_element_type=jnp.float32)
    chi_imag = lax.dot_general(left, jnp.stack(right_imag, axis=1), dims, preferred_element_type=jnp.float32)
    chi_real = chi_real.transpose(1, 0, 2)
    chi_imag = chi_imag.transpose(1, 0, 2)
    return chi_real.astype(jnp.bfloat16), chi_imag.astype(jnp.bfloat16)


def solution(mesh):
    rows, cols = mesh.devices.shape
    grid = Mesh(mesh.devices.reshape(rows, 4, cols // 8, 2), ("row", "x", "y", "core"))
    cols = ("x", "y", "core")
    placed = (P(cols, "row"), P(cols, "row"), P(cols), P(cols), P(), P(), P())
    return jax.shard_map(
        on_device,
        mesh=grid,
        in_specs=placed,
        out_specs=(P(None, "row", cols), P(None, "row", cols)),
        check_vma=False,
    )
```

```python
import jax
import jax.numpy as jnp
from jax import lax
from jax.sharding import Mesh, PartitionSpec as P

CORE_PAIRS = [(0, 1), (1, 0)]


def lookup(indices, table):
    count = table.shape[0]
    picks = indices[:, None] == lax.broadcasted_iota(jnp.int32, (1, count), 1)
    return jnp.sum(jnp.where(picks, table[None, :], 0.0), axis=1)


def shift(value, axis, step):
    size = lax.psum(1, axis)
    return lax.ppermute(value, axis, [(i, (i + step) % size) for i in range(size)])


def ring_gather(block, axis):
    half = block.shape[-1] // 2
    from_minus = shift(block, axis, 1)
    from_plus = shift(block, axis, -1)
    far_first = shift(from_minus[..., :half], axis, 1)
    far_second = shift(from_plus[..., half:], axis, -1)
    return from_plus, far_first, far_second, from_minus


def ring_block(block, axis):
    from_plus, far_first, far_second, from_minus = ring_gather(block, axis)
    far = jnp.concatenate([far_first, far_second], axis=-1)
    return jnp.stack([block, from_plus, far, from_minus])


def on_device(
    matrix_real,
    matrix_imag,
    valence_index,
    conduction_index,
    valence_energy,
    conduction_energy,
    frequency,
):
    cols = ("x", "y", "core")
    nrow = lax.psum(1, "row")
    nx, ny, ncore = lax.psum(1, "x"), lax.psum(1, "y"), lax.psum(1, "core")
    ncol = nx * ny * ncore
    local_pairs, local_g = matrix_real.shape
    pairs = local_pairs * ncol
    width = local_g * nrow // ncol
    both = jnp.stack([matrix_real, matrix_imag])

    copies = jnp.broadcast_to(both[None], (nrow,) + both.shape)
    spread = lax.all_to_all(copies, "row", 0, 0, tiled=True)
    spread = spread.reshape(nrow, 2, local_pairs, local_g // width, width)
    row_real = ring_block(matrix_real, "x")
    col_imag = ring_block(matrix_imag, "y")
    first = jnp.stack([row_real, col_imag])
    first_other = lax.ppermute(first, "core", CORE_PAIRS)
    spread, row_real, col_imag, first = lax.optimization_barrier((spread, row_real, col_imag, first))
    payload = spread.transpose(1, 2, 0, 3, 4).reshape(2, local_pairs, ncol, width)
    bands = jnp.stack([valence_index, conduction_index]).astype(jnp.bfloat16)
    tags = jnp.broadcast_to(bands[:, :, None, None], (2, local_pairs, ncol, 128))
    payload = jnp.concatenate([payload, tags], axis=3)
    column = lax.all_to_all(payload, cols, split_axis=2, concat_axis=1, tiled=True)
    column = column.reshape(2, pairs, width + 128)
    real_plus, real_far_a, real_far_b, real_minus = ring_gather(row_real, "y")
    imag_plus, imag_far_a, imag_far_b, imag_minus = ring_gather(col_imag, "x")
    near = jnp.stack([real_plus, real_minus, imag_plus, imag_minus])
    near_other = lax.ppermute(near, "core", CORE_PAIRS)
    far_a = jnp.stack([real_far_a, imag_far_a])
    far_a_other = lax.ppermute(far_a, "core", CORE_PAIRS)
    far_b = jnp.stack([real_far_b, imag_far_b])
    far_b_other = lax.ppermute(far_b, "core", CORE_PAIRS)
    pieces = []
    for part in range(2):
        for src_first, src_near, src_a, src_b in (
            (first, near, far_a, far_b),
            (first_other, near_other, far_a_other, far_b_other),
        ):
            src_far = jnp.concatenate([src_a[part], src_b[part]], axis=-1)
            for piece in (src_first[part], src_near[2 * part], src_far, src_near[2 * part + 1]):
                pieces.append(piece.reshape(-1, local_g))
    left = jnp.concatenate(pieces, axis=0)

    all_bands = column[:, :, width].astype(jnp.int32)
    gap = lookup(all_bands[1], conduction_energy) - lookup(all_bands[0], valence_energy)
    wide = column[:, :, :width].astype(jnp.float32)
    here = (lax.axis_index("x"), lax.axis_index("y"), lax.axis_index("core"))

    def relative(scaled, order):
        grid = scaled.reshape(nx, ny, ncore, local_pairs, width)
        for axis, start in enumerate(here):
            size = grid.shape[axis]
            doubled = jnp.concatenate([grid, grid], axis=axis)
            grid = lax.dynamic_slice_in_dim(doubled, start, size, axis=axis)
        return grid.transpose(order + (3, 4)).reshape(pairs, width)

    real_order = (2, 1, 0)
    imag_order = (2, 0, 1)
    right_real = []
    right_imag = []
    for index in range(frequency.shape[0]):
        omega = frequency[index]
        weight = 4.0 * gap / (gap * gap + omega * omega)
        scaled_real = (weight[:, None] * wide[0]).astype(jnp.bfloat16)
        scaled_imag = (weight[:, None] * wide[1]).astype(jnp.bfloat16)
        real_a = relative(scaled_real, real_order)
        imag_b = relative(scaled_imag, imag_order)
        real_b = relative(scaled_real, imag_order)
        imag_a = relative(scaled_imag, real_order)
        right_real.append(jnp.concatenate([-real_a, -imag_b], axis=0))
        right_imag.append(jnp.concatenate([-imag_a, real_b], axis=0))
    dims = (((0,), (0,)), ((), ()))
    chi_real = lax.dot_general(left, jnp.stack(right_real, axis=1), dims, preferred_element_type=jnp.float32)
    chi_imag = lax.dot_general(left, jnp.stack(right_imag, axis=1), dims, preferred_element_type=jnp.float32)
    chi_real = chi_real.transpose(1, 0, 2)
    chi_imag = chi_imag.transpose(1, 0, 2)
    return chi_real.astype(jnp.bfloat16), chi_imag.astype(jnp.bfloat16)


def solution(mesh):
    rows, cols = mesh.devices.shape
    grid = Mesh(mesh.devices.reshape(rows, 4, cols // 8, 2), ("row", "x", "y", "core"))
    cols = ("x", "y", "core")
    placed = (P(cols, "row"), P(cols, "row"), P(cols), P(cols), P(), P(), P())
    return jax.shard_map(
        on_device,
        mesh=grid,
        in_specs=placed,
        out_specs=(P(None, "row", cols), P(None, "row", cols)),
        check_vma=False,
    )
```

```python
import jax
import jax.numpy as jnp
from jax import lax
from jax.sharding import Mesh, PartitionSpec as P

CORE_PAIRS = [(0, 1), (1, 0)]


def lookup(indices, table):
    count = table.shape[0]
    picks = indices[:, None] == lax.broadcasted_iota(jnp.int32, (1, count), 1)
    return jnp.sum(jnp.where(picks, table[None, :], 0.0), axis=1)


def shift(value, axis, step):
    size = lax.psum(1, axis)
    return lax.ppermute(value, axis, [(i, (i + step) % size) for i in range(size)])


def ring_gather(block, axis):
    half = block.shape[-1] // 2
    from_minus = shift(block, axis, 1)
    from_plus = shift(block, axis, -1)
    far_first = shift(from_minus[..., :half], axis, 1)
    far_second = shift(from_plus[..., half:], axis, -1)
    far = jnp.concatenate([far_first, far_second], axis=-1)
    return from_plus, far, from_minus


def on_device(
    matrix_real,
    matrix_imag,
    valence_index,
    conduction_index,
    valence_energy,
    conduction_energy,
    frequency,
):
    cols = ("x", "y", "core")
    nrow = lax.psum(1, "row")
    nx, ny, ncore = lax.psum(1, "x"), lax.psum(1, "y"), lax.psum(1, "core")
    ncol = nx * ny * ncore
    local_pairs, local_g = matrix_real.shape
    pairs = local_pairs * ncol
    width = local_g * nrow // ncol
    both = jnp.stack([matrix_real, matrix_imag])

    copies = jnp.broadcast_to(both[None], (nrow,) + both.shape)
    spread = lax.all_to_all(copies, "row", 0, 0, tiled=True)
    spread = spread.reshape(nrow, 2, local_pairs, local_g // width, width)
    row_real = jnp.stack((matrix_real,) + ring_gather(matrix_real, "x"))
    col_imag = jnp.stack((matrix_imag,) + ring_gather(matrix_imag, "y"))
    first = jnp.stack([row_real, col_imag])
    first_other = lax.ppermute(first, "core", CORE_PAIRS)
    spread, row_real, col_imag, first = lax.optimization_barrier((spread, row_real, col_imag, first))
    payload = spread.transpose(1, 2, 0, 3, 4).reshape(2, local_pairs, ncol, width)
    bands = jnp.stack([valence_index, conduction_index]).astype(jnp.bfloat16)
    tags = jnp.broadcast_to(bands[:, :, None, None], (2, local_pairs, ncol, 128))
    payload = jnp.concatenate([payload, tags], axis=3)
    column = lax.all_to_all(payload, cols, split_axis=2, concat_axis=1, tiled=True)
    column = column.reshape(2, pairs, width + 128)
    real_plus, real_far, real_minus = ring_gather(row_real, "y")
    imag_plus, imag_far, imag_minus = ring_gather(col_imag, "x")
    near = lax.optimization_barrier(jnp.stack([real_plus, real_minus, imag_plus, imag_minus]))
    near_other = lax.ppermute(near, "core", CORE_PAIRS)
    far = lax.optimization_barrier(jnp.stack([real_far, imag_far]))
    far_other = lax.ppermute(far, "core", CORE_PAIRS)
    parts = []
    for part in range(2):
        for src_first, src_near, src_far in ((first, near, far), (first_other, near_other, far_other)):
            parts.append(
                jnp.stack([src_first[part], src_near[2 * part], src_far[part], src_near[2 * part + 1]])
            )
    left = jnp.stack(parts).reshape(2 * pairs, local_g)

    all_bands = column[:, :, width].astype(jnp.int32)
    gap = lookup(all_bands[1], conduction_energy) - lookup(all_bands[0], valence_energy)
    wide = column[:, :, :width].astype(jnp.float32)
    here = (lax.axis_index("x"), lax.axis_index("y"), lax.axis_index("core"))

    def relative(scaled, order):
        grid = scaled.reshape(nx, ny, ncore, local_pairs, width)
        for axis, start in enumerate(here):
            size = grid.shape[axis]
            doubled = jnp.concatenate([grid, grid], axis=axis)
            grid = lax.dynamic_slice_in_dim(doubled, start, size, axis=axis)
        return grid.transpose(order + (3, 4)).reshape(pairs, width)

    real_order = (2, 1, 0)
    imag_order = (2, 0, 1)
    right_real = []
    right_imag = []
    for index in range(frequency.shape[0]):
        omega = frequency[index]
        weight = 4.0 * gap / (gap * gap + omega * omega)
        scaled_real = (weight[:, None] * wide[0]).astype(jnp.bfloat16)
        scaled_imag = (weight[:, None] * wide[1]).astype(jnp.bfloat16)
        real_a = relative(scaled_real, real_order)
        imag_b = relative(scaled_imag, imag_order)
        real_b = relative(scaled_real, imag_order)
        imag_a = relative(scaled_imag, real_order)
        right_real.append(jnp.concatenate([-real_a, -imag_b], axis=0))
        right_imag.append(jnp.concatenate([-imag_a, real_b], axis=0))
    dims = (((0,), (0,)), ((), ()))
    chi_real = lax.dot_general(left, jnp.stack(right_real, axis=1), dims, preferred_element_type=jnp.float32)
    chi_imag = lax.dot_general(left, jnp.stack(right_imag, axis=1), dims, preferred_element_type=jnp.float32)
    chi_real = chi_real.transpose(1, 0, 2)
    chi_imag = chi_imag.transpose(1, 0, 2)
    return chi_real.astype(jnp.bfloat16), chi_imag.astype(jnp.bfloat16)


def solution(mesh):
    rows, cols = mesh.devices.shape
    grid = Mesh(mesh.devices.reshape(rows, 4, cols // 8, 2), ("row", "x", "y", "core"))
    cols = ("x", "y", "core")
    placed = (P(cols, "row"), P(cols, "row"), P(cols), P(cols), P(), P(), P())
    return jax.shard_map(
        on_device,
        mesh=grid,
        in_specs=placed,
        out_specs=(P(None, "row", cols), P(None, "row", cols)),
        check_vma=False,
    )
```

```python
import jax
import jax.numpy as jnp
from jax import lax
from jax.sharding import Mesh, PartitionSpec as P

CORE_PAIRS = [(0, 1), (1, 0)]


def lookup(indices, table):
    count = table.shape[0]
    picks = indices[:, None] == lax.broadcasted_iota(jnp.int32, (1, count), 1)
    return jnp.sum(jnp.where(picks, table[None, :], 0.0), axis=1)


def shift(value, axis, step):
    size = lax.psum(1, axis)
    return lax.ppermute(value, axis, [(i, (i + step) % size) for i in range(size)])


def ring_gather(block, axis):
    half = block.shape[-1] // 2
    from_minus = shift(block, axis, 1)
    from_plus = shift(block, axis, -1)
    far_first = shift(from_minus[..., :half], axis, 1)
    far_second = shift(from_plus[..., half:], axis, -1)
    far = jnp.concatenate([far_first, far_second], axis=-1)
    return from_plus, far, from_minus


def on_device(
    matrix_real,
    matrix_imag,
    valence_index,
    conduction_index,
    valence_energy,
    conduction_energy,
    frequency,
):
    cols = ("x", "y", "core")
    nrow = lax.psum(1, "row")
    nx, ny, ncore = lax.psum(1, "x"), lax.psum(1, "y"), lax.psum(1, "core")
    ncol = nx * ny * ncore
    local_pairs, local_g = matrix_real.shape
    pairs = local_pairs * ncol
    width = local_g * nrow // ncol
    both = jnp.stack([matrix_real, matrix_imag])

    spread = lax.all_gather(both, "row", axis=0)
    spread = spread.reshape(nrow, 2, local_pairs, local_g // width, width)
    row_real = jnp.stack((matrix_real,) + ring_gather(matrix_real, "x"))
    col_imag = jnp.stack((matrix_imag,) + ring_gather(matrix_imag, "y"))
    first = jnp.stack([row_real, col_imag])
    first_other = lax.ppermute(first, "core", CORE_PAIRS)
    spread, row_real, col_imag, first = lax.optimization_barrier((spread, row_real, col_imag, first))
    payload = spread.transpose(1, 2, 0, 3, 4).reshape(2, local_pairs, ncol, width)
    bands = jnp.stack([valence_index, conduction_index]).astype(jnp.bfloat16)
    tags = jnp.broadcast_to(bands[:, :, None, None], (2, local_pairs, ncol, 128))
    payload = jnp.concatenate([payload, tags], axis=3)
    column = lax.all_to_all(payload, cols, split_axis=2, concat_axis=1, tiled=True)
    column = column.reshape(2, pairs, width + 128)
    real_plus, real_far, real_minus = ring_gather(row_real, "y")
    imag_plus, imag_far, imag_minus = ring_gather(col_imag, "x")
    near = jnp.stack([real_plus, real_minus, imag_plus, imag_minus])
    near_other = lax.ppermute(near, "core", CORE_PAIRS)
    far = jnp.stack([real_far, imag_far])
    far_other = lax.ppermute(far, "core", CORE_PAIRS)
    parts = []
    for part in range(2):
        for src_first, src_near, src_far in ((first, near, far), (first_other, near_other, far_other)):
            parts.append(
                jnp.stack([src_first[part], src_near[2 * part], src_far[part], src_near[2 * part + 1]])
            )
    left = jnp.stack(parts).reshape(2 * pairs, local_g)

    all_bands = column[:, :, width].astype(jnp.int32)
    gap = lookup(all_bands[1], conduction_energy) - lookup(all_bands[0], valence_energy)
    wide = column[:, :, :width].astype(jnp.float32)
    here = (lax.axis_index("x"), lax.axis_index("y"), lax.axis_index("core"))

    def relative(scaled, order):
        grid = scaled.reshape(nx, ny, ncore, local_pairs, width)
        for axis, start in enumerate(here):
            size = grid.shape[axis]
            doubled = jnp.concatenate([grid, grid], axis=axis)
            grid = lax.dynamic_slice_in_dim(doubled, start, size, axis=axis)
        return grid.transpose(order + (3, 4)).reshape(pairs, width)

    real_order = (2, 1, 0)
    imag_order = (2, 0, 1)
    right_real = []
    right_imag = []
    for index in range(frequency.shape[0]):
        omega = frequency[index]
        weight = 4.0 * gap / (gap * gap + omega * omega)
        scaled_real = (weight[:, None] * wide[0]).astype(jnp.bfloat16)
        scaled_imag = (weight[:, None] * wide[1]).astype(jnp.bfloat16)
        real_a = relative(scaled_real, real_order)
        imag_b = relative(scaled_imag, imag_order)
        real_b = relative(scaled_real, imag_order)
        imag_a = relative(scaled_imag, real_order)
        right_real.append(jnp.concatenate([-real_a, -imag_b], axis=0))
        right_imag.append(jnp.concatenate([-imag_a, real_b], axis=0))
    dims = (((0,), (0,)), ((), ()))
    chi_real = lax.dot_general(left, jnp.stack(right_real, axis=1), dims, preferred_element_type=jnp.float32)
    chi_imag = lax.dot_general(left, jnp.stack(right_imag, axis=1), dims, preferred_element_type=jnp.float32)
    chi_real = chi_real.transpose(1, 0, 2)
    chi_imag = chi_imag.transpose(1, 0, 2)
    return chi_real.astype(jnp.bfloat16), chi_imag.astype(jnp.bfloat16)


def solution(mesh):
    rows, cols = mesh.devices.shape
    grid = Mesh(mesh.devices.reshape(rows, 4, cols // 8, 2), ("row", "x", "y", "core"))
    cols = ("x", "y", "core")
    placed = (P(cols, "row"), P(cols, "row"), P(cols), P(cols), P(), P(), P())
    return jax.shard_map(
        on_device,
        mesh=grid,
        in_specs=placed,
        out_specs=(P(None, "row", cols), P(None, "row", cols)),
        check_vma=False,
    )
```

```python
import jax
import jax.numpy as jnp
from jax import lax
from jax.sharding import Mesh, PartitionSpec as P

CORE_PAIRS = [(0, 1), (1, 0)]


def lookup(indices, table):
    count = table.shape[0]
    picks = indices[:, None] == lax.broadcasted_iota(jnp.int32, (1, count), 1)
    return jnp.sum(jnp.where(picks, table[None, :], 0.0), axis=1)


def shift(value, axis, step):
    size = lax.psum(1, axis)
    return lax.ppermute(value, axis, [(i, (i + step) % size) for i in range(size)])


def ring_gather(block, axis):
    half = block.shape[-1] // 2
    from_minus = shift(block, axis, 1)
    from_plus = shift(block, axis, -1)
    far_first = shift(from_minus[..., :half], axis, 1)
    far_second = shift(from_plus[..., half:], axis, -1)
    far = jnp.concatenate([far_first, far_second], axis=-1)
    return from_plus, far, from_minus


def on_device(
    matrix_real,
    matrix_imag,
    valence_index,
    conduction_index,
    valence_energy,
    conduction_energy,
    frequency,
):
    cols = ("x", "y", "core")
    nrow = lax.psum(1, "row")
    nx, ny, ncore = lax.psum(1, "x"), lax.psum(1, "y"), lax.psum(1, "core")
    ncol = nx * ny * ncore
    local_pairs, local_g = matrix_real.shape
    pairs = local_pairs * ncol
    width = local_g * nrow // ncol
    both = jnp.stack([matrix_real, matrix_imag])

    copies = jnp.broadcast_to(both[None], (nrow,) + both.shape)
    spread = lax.all_to_all(copies, "row", 0, 0, tiled=True)
    spread = spread.reshape(nrow, 2, local_pairs, local_g // width, width)
    row_real = jnp.stack((matrix_real,) + ring_gather(matrix_real, "x"))
    col_imag = jnp.stack((matrix_imag,) + ring_gather(matrix_imag, "y"))
    first = jnp.stack([row_real, col_imag])
    first_other = lax.ppermute(first, "core", CORE_PAIRS)
    spread, row_real, col_imag, first = lax.optimization_barrier((spread, row_real, col_imag, first))
    payload = spread.transpose(1, 2, 0, 3, 4).reshape(2, local_pairs, ncol, width)
    bands = jnp.stack([valence_index, conduction_index]).astype(jnp.bfloat16)
    tags = jnp.broadcast_to(bands[:, :, None, None], (2, local_pairs, ncol, 128))
    payload = jnp.concatenate([payload, tags], axis=3)
    column = lax.all_to_all(payload, cols, split_axis=2, concat_axis=1, tiled=True)
    column = column.reshape(2, pairs, width + 128)
    real_plus, real_far, real_minus = ring_gather(row_real, "y")
    imag_plus, imag_far, imag_minus = ring_gather(col_imag, "x")
    near = jnp.stack([real_plus, real_minus, imag_plus, imag_minus])
    near_other = lax.ppermute(near, "core", CORE_PAIRS)
    far = jnp.stack([real_far, imag_far])
    far_other = lax.ppermute(far, "core", CORE_PAIRS)
    buffers = (first, near, far, first_other, near_other, far_other)
    left = jnp.concatenate([piece.reshape(-1, local_pairs, local_g) for piece in buffers], axis=0)
    left = left.reshape(2 * pairs, local_g)

    all_bands = column[:, :, width].astype(jnp.int32)
    gap = lookup(all_bands[1], conduction_energy) - lookup(all_bands[0], valence_energy)
    wide = column[:, :, :width].astype(jnp.float32)
    here = (lax.axis_index("x"), lax.axis_index("y"), lax.axis_index("core"))

    def relative(scaled, order):
        grid = scaled.reshape(nx, ny, ncore, local_pairs, width)
        for axis, start in enumerate(here):
            size = grid.shape[axis]
            doubled = jnp.concatenate([grid, grid], axis=axis)
            grid = lax.dynamic_slice_in_dim(doubled, start, size, axis=axis)
        return grid.transpose(order + (3, 4)).reshape(pairs, width)

    real_order = (2, 1, 0)
    imag_order = (2, 0, 1)
    slots = ((0, 0), (1, 0), (0, 1), (0, 3), (1, 1), (1, 3), (0, 2), (1, 2))

    def arrange(real_rows, imag_rows):
        grids = [rows.reshape(ncore, 4, 4 * local_pairs, width) for rows in (real_rows, imag_rows)]
        return jnp.stack([grids[part][:, outer] for part, outer in slots], axis=1).reshape(pairs * 2, width)

    right_real = []
    right_imag = []
    for index in range(frequency.shape[0]):
        omega = frequency[index]
        weight = 4.0 * gap / (gap * gap + omega * omega)
        scaled_real = (weight[:, None] * wide[0]).astype(jnp.bfloat16)
        scaled_imag = (weight[:, None] * wide[1]).astype(jnp.bfloat16)
        real_a = relative(scaled_real, real_order)
        imag_b = relative(scaled_imag, imag_order)
        real_b = relative(scaled_real, imag_order)
        imag_a = relative(scaled_imag, real_order)
        right_real.append(arrange(-real_a, -imag_b))
        right_imag.append(arrange(-imag_a, real_b))
    dims = (((0,), (0,)), ((), ()))
    chi_real = lax.dot_general(left, jnp.stack(right_real, axis=1), dims, preferred_element_type=jnp.float32)
    chi_imag = lax.dot_general(left, jnp.stack(right_imag, axis=1), dims, preferred_element_type=jnp.float32)
    chi_real = chi_real.transpose(1, 0, 2)
    chi_imag = chi_imag.transpose(1, 0, 2)
    return chi_real.astype(jnp.bfloat16), chi_imag.astype(jnp.bfloat16)


def solution(mesh):
    rows, cols = mesh.devices.shape
    grid = Mesh(mesh.devices.reshape(rows, 4, cols // 8, 2), ("row", "x", "y", "core"))
    cols = ("x", "y", "core")
    placed = (P(cols, "row"), P(cols, "row"), P(cols), P(cols), P(), P(), P())
    return jax.shard_map(
        on_device,
        mesh=grid,
        in_specs=placed,
        out_specs=(P(None, "row", cols), P(None, "row", cols)),
        check_vma=False,
    )
```

```python
import jax
import jax.numpy as jnp
from jax import lax
from jax.sharding import Mesh, PartitionSpec as P

CORE_PAIRS = [(0, 1), (1, 0)]


def lookup(indices, table):
    count = table.shape[0]
    picks = indices[:, None] == lax.broadcasted_iota(jnp.int32, (1, count), 1)
    return jnp.sum(jnp.where(picks, table[None, :], 0.0), axis=1)


def shift(value, axis, step):
    size = lax.psum(1, axis)
    return lax.ppermute(value, axis, [(i, (i + step) % size) for i in range(size)])


def ring_gather(block, axis):
    half = block.shape[-1] // 2
    from_minus = shift(block, axis, 1)
    from_plus = shift(block, axis, -1)
    far_first = shift(from_minus[..., :half], axis, 1)
    far_second = shift(from_plus[..., half:], axis, -1)
    far = jnp.concatenate([far_first, far_second], axis=-1)
    return from_plus, far, from_minus


def on_device(
    matrix_real,
    matrix_imag,
    valence_index,
    conduction_index,
    valence_energy,
    conduction_energy,
    frequency,
):
    cols = ("x", "y", "core")
    nrow = lax.psum(1, "row")
    nx, ny, ncore = lax.psum(1, "x"), lax.psum(1, "y"), lax.psum(1, "core")
    ncol = nx * ny * ncore
    local_pairs, local_g = matrix_real.shape
    pairs = local_pairs * ncol
    width = local_g * nrow // ncol
    both = jnp.stack([matrix_real, matrix_imag])

    copies = jnp.broadcast_to(both[None], (nrow,) + both.shape)
    spread = lax.all_to_all(copies, "row", 0, 0, tiled=True)
    spread = spread.reshape(nrow, 2, local_pairs, local_g // width, width)
    row_real = jnp.stack((matrix_real,) + ring_gather(matrix_real, "x"))
    col_imag = jnp.stack((matrix_imag,) + ring_gather(matrix_imag, "y"))
    first = jnp.stack([row_real, col_imag])
    first_other = lax.ppermute(first, "core", CORE_PAIRS)
    spread, row_real, col_imag, first = lax.optimization_barrier((spread, row_real, col_imag, first))
    payload = spread.transpose(0, 3, 1, 2, 4).reshape(ncol, 2, local_pairs, width)
    bands = jnp.stack([valence_index, conduction_index]).astype(jnp.bfloat16)
    tags = jnp.broadcast_to(bands[None, :, :, None], (ncol, 2, local_pairs, 128))
    payload = jnp.concatenate([payload, tags], axis=3)
    column = lax.all_to_all(payload, cols, split_axis=0, concat_axis=0, tiled=True)
    column = column.transpose(1, 0, 2, 3).reshape(2, pairs, width + 128)
    real_plus, real_far, real_minus = ring_gather(row_real, "y")
    imag_plus, imag_far, imag_minus = ring_gather(col_imag, "x")
    near = jnp.stack([real_plus, real_minus, imag_plus, imag_minus])
    near_other = lax.ppermute(near, "core", CORE_PAIRS)
    far = jnp.stack([real_far, imag_far])
    far_other = lax.ppermute(far, "core", CORE_PAIRS)
    parts = []
    for part in range(2):
        for src_first, src_near, src_far in ((first, near, far), (first_other, near_other, far_other)):
            parts.append(
                jnp.stack([src_first[part], src_near[2 * part], src_far[part], src_near[2 * part + 1]])
            )
    left = jnp.stack(parts).reshape(2 * pairs, local_g)

    all_bands = column[:, :, width].astype(jnp.int32)
    gap = lookup(all_bands[1], conduction_energy) - lookup(all_bands[0], valence_energy)
    wide = column[:, :, :width].astype(jnp.float32)
    here = (lax.axis_index("x"), lax.axis_index("y"), lax.axis_index("core"))

    def relative(scaled, order):
        grid = scaled.reshape(nx, ny, ncore, local_pairs, width)
        for axis, start in enumerate(here):
            size = grid.shape[axis]
            doubled = jnp.concatenate([grid, grid], axis=axis)
            grid = lax.dynamic_slice_in_dim(doubled, start, size, axis=axis)
        return grid.transpose(order + (3, 4)).reshape(pairs, width)

    real_order = (2, 1, 0)
    imag_order = (2, 0, 1)
    right_real = []
    right_imag = []
    for index in range(frequency.shape[0]):
        omega = frequency[index]
        weight = 4.0 * gap / (gap * gap + omega * omega)
        scaled_real = (weight[:, None] * wide[0]).astype(jnp.bfloat16)
        scaled_imag = (weight[:, None] * wide[1]).astype(jnp.bfloat16)
        real_a = relative(scaled_real, real_order)
        imag_b = relative(scaled_imag, imag_order)
        real_b = relative(scaled_real, imag_order)
        imag_a = relative(scaled_imag, real_order)
        right_real.append(jnp.concatenate([-real_a, -imag_b], axis=0))
        right_imag.append(jnp.concatenate([-imag_a, real_b], axis=0))
    dims = (((0,), (0,)), ((), ()))
    chi_real = lax.dot_general(left, jnp.stack(right_real, axis=1), dims, preferred_element_type=jnp.float32)
    chi_imag = lax.dot_general(left, jnp.stack(right_imag, axis=1), dims, preferred_element_type=jnp.float32)
    chi_real = chi_real.transpose(1, 0, 2)
    chi_imag = chi_imag.transpose(1, 0, 2)
    return chi_real.astype(jnp.bfloat16), chi_imag.astype(jnp.bfloat16)


def solution(mesh):
    rows, cols = mesh.devices.shape
    grid = Mesh(mesh.devices.reshape(rows, 4, cols // 8, 2), ("row", "x", "y", "core"))
    cols = ("x", "y", "core")
    placed = (P(cols, "row"), P(cols, "row"), P(cols), P(cols), P(), P(), P())
    return jax.shard_map(
        on_device,
        mesh=grid,
        in_specs=placed,
        out_specs=(P(None, "row", cols), P(None, "row", cols)),
        check_vma=False,
    )
```

```python
import jax
import jax.numpy as jnp
from jax import lax
from jax.sharding import Mesh, PartitionSpec as P

CORE_PAIRS = [(0, 1), (1, 0)]


def lookup(indices, table):
    count = table.shape[0]
    picks = indices[:, None] == lax.broadcasted_iota(jnp.int32, (1, count), 1)
    return jnp.sum(jnp.where(picks, table[None, :], 0.0), axis=1)


def shift(value, axis, step):
    size = lax.psum(1, axis)
    return lax.ppermute(value, axis, [(i, (i + step) % size) for i in range(size)])


def ring_gather(block, axis):
    half = block.shape[-1] // 2
    from_minus = shift(block, axis, 1)
    from_plus = shift(block, axis, -1)
    far_first = shift(from_minus[..., :half], axis, 1)
    far_second = shift(from_plus[..., half:], axis, -1)
    far = jnp.concatenate([far_first, far_second], axis=-1)
    return from_plus, far, from_minus


def ring_direct(block, axis):
    return jnp.stack([block, shift(block, axis, -1), shift(block, axis, 2), shift(block, axis, 1)])


def on_device(
    matrix_real,
    matrix_imag,
    valence_index,
    conduction_index,
    valence_energy,
    conduction_energy,
    frequency,
):
    cols = ("x", "y", "core")
    nrow = lax.psum(1, "row")
    nx, ny, ncore = lax.psum(1, "x"), lax.psum(1, "y"), lax.psum(1, "core")
    ncol = nx * ny * ncore
    local_pairs, local_g = matrix_real.shape
    pairs = local_pairs * ncol
    width = local_g * nrow // ncol
    both = jnp.stack([matrix_real, matrix_imag])

    copies = jnp.broadcast_to(both[None], (nrow,) + both.shape)
    spread = lax.all_to_all(copies, "row", 0, 0, tiled=True)
    spread = spread.reshape(nrow, 2, local_pairs, local_g // width, width)
    row_real = ring_direct(matrix_real, "x")
    col_imag = ring_direct(matrix_imag, "y")
    first = jnp.stack([row_real, col_imag])
    first_other = lax.ppermute(first, "core", CORE_PAIRS)
    spread, row_real, col_imag, first = lax.optimization_barrier((spread, row_real, col_imag, first))
    payload = spread.transpose(0, 3, 1, 2, 4).reshape(ncol, 2, local_pairs, width)
    bands = jnp.stack([valence_index, conduction_index]).astype(jnp.bfloat16)
    tags = jnp.broadcast_to(bands[None, :, :, None], (ncol, 2, local_pairs, 128))
    payload = jnp.concatenate([payload, tags], axis=3)
    column = lax.all_to_all(payload, cols, split_axis=0, concat_axis=0, tiled=True)
    column = column.transpose(1, 0, 2, 3).reshape(2, pairs, width + 128)
    real_plus, real_far, real_minus = ring_gather(row_real, "y")
    imag_plus, imag_far, imag_minus = ring_gather(col_imag, "x")
    near = jnp.stack([real_plus, real_minus, imag_plus, imag_minus])
    near_other = lax.ppermute(near, "core", CORE_PAIRS)
    far = jnp.stack([real_far, imag_far])
    far_other = lax.ppermute(far, "core", CORE_PAIRS)
    parts = []
    for part in range(2):
        for src_first, src_near, src_far in ((first, near, far), (first_other, near_other, far_other)):
            parts.append(
                jnp.stack([src_first[part], src_near[2 * part], src_far[part], src_near[2 * part + 1]])
            )
    left = jnp.stack(parts).reshape(2 * pairs, local_g)

    all_bands = column[:, :, width].astype(jnp.int32)
    gap = lookup(all_bands[1], conduction_energy) - lookup(all_bands[0], valence_energy)
    wide = column[:, :, :width].astype(jnp.float32)
    here = (lax.axis_index("x"), lax.axis_index("y"), lax.axis_index("core"))

    def relative(scaled, order):
        grid = scaled.reshape(nx, ny, ncore, local_pairs, width)
        for axis, start in enumerate(here):
            size = grid.shape[axis]
            doubled = jnp.concatenate([grid, grid], axis=axis)
            grid = lax.dynamic_slice_in_dim(doubled, start, size, axis=axis)
        return grid.transpose(order + (3, 4)).reshape(pairs, width)

    real_order = (2, 1, 0)
    imag_order = (2, 0, 1)
    right_real = []
    right_imag = []
    for index in range(frequency.shape[0]):
        omega = frequency[index]
        weight = 4.0 * gap / (gap * gap + omega * omega)
        scaled_real = (weight[:, None] * wide[0]).astype(jnp.bfloat16)
        scaled_imag = (weight[:, None] * wide[1]).astype(jnp.bfloat16)
        real_a = relative(scaled_real, real_order)
        imag_b = relative(scaled_imag, imag_order)
        real_b = relative(scaled_real, imag_order)
        imag_a = relative(scaled_imag, real_order)
        right_real.append(jnp.concatenate([-real_a, -imag_b], axis=0))
        right_imag.append(jnp.concatenate([-imag_a, real_b], axis=0))
    dims = (((0,), (0,)), ((), ()))
    chi_real = lax.dot_general(left, jnp.stack(right_real, axis=1), dims, preferred_element_type=jnp.float32)
    chi_imag = lax.dot_general(left, jnp.stack(right_imag, axis=1), dims, preferred_element_type=jnp.float32)
    chi_real = chi_real.transpose(1, 0, 2)
    chi_imag = chi_imag.transpose(1, 0, 2)
    return chi_real.astype(jnp.bfloat16), chi_imag.astype(jnp.bfloat16)


def solution(mesh):
    rows, cols = mesh.devices.shape
    grid = Mesh(mesh.devices.reshape(rows, 4, cols // 8, 2), ("row", "x", "y", "core"))
    cols = ("x", "y", "core")
    placed = (P(cols, "row"), P(cols, "row"), P(cols), P(cols), P(), P(), P())
    return jax.shard_map(
        on_device,
        mesh=grid,
        in_specs=placed,
        out_specs=(P(None, "row", cols), P(None, "row", cols)),
        check_vma=False,
    )
```

```python
import jax
import jax.numpy as jnp
from jax import lax
from jax.sharding import Mesh, PartitionSpec as P

CORE_PAIRS = [(0, 1), (1, 0)]


def lookup(indices, table):
    count = table.shape[0]
    picks = indices[:, None] == lax.broadcasted_iota(jnp.int32, (1, count), 1)
    return jnp.sum(jnp.where(picks, table[None, :], 0.0), axis=1)


def shift(value, axis, step):
    size = lax.psum(1, axis)
    return lax.ppermute(value, axis, [(i, (i + step) % size) for i in range(size)])


def ring_gather(block, axis):
    half = block.shape[0] // 2
    from_minus = shift(block, axis, 1)
    from_plus = shift(block, axis, -1)
    far_first = shift(from_minus[:half], axis, 1)
    far_second = shift(from_plus[half:], axis, -1)
    far = jnp.concatenate([far_first, far_second], axis=0)
    return from_plus, far, from_minus


def ring_direct(block, axis):
    return jnp.stack([block, shift(block, axis, -1), shift(block, axis, 2), shift(block, axis, 1)])


def on_device(
    matrix_real,
    matrix_imag,
    valence_index,
    conduction_index,
    valence_energy,
    conduction_energy,
    frequency,
):
    cols = ("x", "y", "core")
    nrow = lax.psum(1, "row")
    nx, ny, ncore = lax.psum(1, "x"), lax.psum(1, "y"), lax.psum(1, "core")
    ncol = nx * ny * ncore
    local_pairs, local_g = matrix_real.shape
    pairs = local_pairs * ncol
    width = local_g * nrow // ncol
    both = jnp.stack([matrix_real, matrix_imag])

    copies = jnp.broadcast_to(both[None], (nrow,) + both.shape)
    spread = lax.all_to_all(copies, "row", 0, 0, tiled=True)
    spread = spread.reshape(nrow, 2, local_pairs, local_g // width, width)
    row_real = ring_direct(matrix_real, "x")
    col_imag = ring_direct(matrix_imag, "y")
    first = jnp.stack([row_real, col_imag])
    first_other = lax.ppermute(first, "core", CORE_PAIRS)
    spread, row_real, col_imag, first = lax.optimization_barrier((spread, row_real, col_imag, first))
    payload = spread.transpose(0, 3, 1, 2, 4).reshape(ncol, 2, local_pairs, width)
    bands = jnp.stack([valence_index, conduction_index]).astype(jnp.bfloat16)
    tags = jnp.broadcast_to(bands[None, :, :, None], (ncol, 2, local_pairs, 128))
    payload = jnp.concatenate([payload, tags], axis=3)
    column = lax.all_to_all(payload, cols, split_axis=0, concat_axis=0, tiled=True)
    column = column.transpose(1, 0, 2, 3).reshape(2, pairs, width + 128)
    real_plus, real_far, real_minus = ring_gather(row_real, "y")
    imag_plus, imag_far, imag_minus = ring_gather(col_imag, "x")
    near = jnp.stack([real_plus, real_minus, imag_plus, imag_minus])
    near_other = lax.ppermute(near, "core", CORE_PAIRS)
    far = jnp.stack([real_far, imag_far])
    far_other = lax.ppermute(far, "core", CORE_PAIRS)
    parts = []
    for part in range(2):
        for src_first, src_near, src_far in ((first, near, far), (first_other, near_other, far_other)):
            parts.append(
                jnp.stack([src_first[part], src_near[2 * part], src_far[part], src_near[2 * part + 1]])
            )
    left = jnp.stack(parts).reshape(2 * pairs, local_g)

    all_bands = column[:, :, width].astype(jnp.int32)
    gap = lookup(all_bands[1], conduction_energy) - lookup(all_bands[0], valence_energy)
    wide = column[:, :, :width].astype(jnp.float32)
    here = (lax.axis_index("x"), lax.axis_index("y"), lax.axis_index("core"))

    def relative(scaled, order):
        grid = scaled.reshape(nx, ny, ncore, local_pairs, width)
        for axis, start in enumerate(here):
            size = grid.shape[axis]
            doubled = jnp.concatenate([grid, grid], axis=axis)
            grid = lax.dynamic_slice_in_dim(doubled, start, size, axis=axis)
        return grid.transpose(order + (3, 4)).reshape(pairs, width)

    real_order = (2, 1, 0)
    imag_order = (2, 0, 1)
    right_real = []
    right_imag = []
    for index in range(frequency.shape[0]):
        omega = frequency[index]
        weight = 4.0 * gap / (gap * gap + omega * omega)
        scaled_real = (weight[:, None] * wide[0]).astype(jnp.bfloat16)
        scaled_imag = (weight[:, None] * wide[1]).astype(jnp.bfloat16)
        real_a = relative(scaled_real, real_order)
        imag_b = relative(scaled_imag, imag_order)
        real_b = relative(scaled_real, imag_order)
        imag_a = relative(scaled_imag, real_order)
        right_real.append(jnp.concatenate([-real_a, -imag_b], axis=0))
        right_imag.append(jnp.concatenate([-imag_a, real_b], axis=0))
    dims = (((0,), (0,)), ((), ()))
    chi_real = lax.dot_general(left, jnp.stack(right_real, axis=1), dims, preferred_element_type=jnp.float32)
    chi_imag = lax.dot_general(left, jnp.stack(right_imag, axis=1), dims, preferred_element_type=jnp.float32)
    chi_real = chi_real.transpose(1, 0, 2)
    chi_imag = chi_imag.transpose(1, 0, 2)
    return chi_real.astype(jnp.bfloat16), chi_imag.astype(jnp.bfloat16)


def solution(mesh):
    rows, cols = mesh.devices.shape
    grid = Mesh(mesh.devices.reshape(rows, 4, cols // 8, 2), ("row", "x", "y", "core"))
    cols = ("x", "y", "core")
    placed = (P(cols, "row"), P(cols, "row"), P(cols), P(cols), P(), P(), P())
    return jax.shard_map(
        on_device,
        mesh=grid,
        in_specs=placed,
        out_specs=(P(None, "row", cols), P(None, "row", cols)),
        check_vma=False,
    )
```

```python
import jax
import jax.numpy as jnp
from jax import lax
from jax.sharding import Mesh, PartitionSpec as P

CORE_PAIRS = [(0, 1), (1, 0)]


def lookup(indices, table):
    count = table.shape[0]
    picks = indices[:, None] == lax.broadcasted_iota(jnp.int32, (1, count), 1)
    return jnp.sum(jnp.where(picks, table[None, :], 0.0), axis=1)


def shift(value, axis, step):
    size = lax.psum(1, axis)
    return lax.ppermute(value, axis, [(i, (i + step) % size) for i in range(size)])


def ring_gather(block, axis):
    half = block.shape[-1] // 2
    from_minus = shift(block, axis, 1)
    from_plus = shift(block, axis, -1)
    far_first = shift(from_minus[..., :half], axis, 1)
    far_second = shift(from_plus[..., half:], axis, -1)
    far = jnp.concatenate([far_first, far_second], axis=-1)
    return from_plus, far, from_minus


def ring_direct(block, axis):
    return jnp.stack([block, shift(block, axis, -1), shift(block, axis, 2), shift(block, axis, 1)])


def on_device(
    matrix_real,
    matrix_imag,
    valence_index,
    conduction_index,
    valence_energy,
    conduction_energy,
    frequency,
):
    cols = ("x", "y", "core")
    nrow = lax.psum(1, "row")
    nx, ny, ncore = lax.psum(1, "x"), lax.psum(1, "y"), lax.psum(1, "core")
    ncol = nx * ny * ncore
    local_pairs, local_g = matrix_real.shape
    pairs = local_pairs * ncol
    width = local_g * nrow // ncol
    both = jnp.stack([matrix_real, matrix_imag])

    copies = jnp.broadcast_to(both[None], (nrow,) + both.shape)
    spread = lax.all_to_all(copies, "row", 0, 0, tiled=True)
    spread = spread.reshape(nrow, 2, local_pairs, local_g // width, width)
    row_real = ring_direct(matrix_real, "x")
    col_imag = ring_direct(matrix_imag, "y")
    first = jnp.stack([row_real, col_imag])
    first_other = lax.ppermute(first, "core", CORE_PAIRS)
    spread, row_real, col_imag, first = lax.optimization_barrier((spread, row_real, col_imag, first))
    payload = spread.transpose(0, 3, 1, 2, 4).reshape(ncol, 2, local_pairs, width)
    bands = jnp.stack([valence_index, conduction_index]).astype(jnp.bfloat16)
    tags = jnp.broadcast_to(bands[None, :, :, None], (ncol, 2, local_pairs, 128))
    payload = jnp.concatenate([payload, tags], axis=3)
    column = lax.all_to_all(payload, cols, split_axis=0, concat_axis=0, tiled=True)
    column = column.transpose(1, 0, 2, 3).reshape(2, pairs, width + 128)
    real_plus, real_far, real_minus = ring_gather(row_real, "y")
    imag_plus, imag_far, imag_minus = ring_gather(col_imag, "x")
    near = jnp.stack([real_plus, real_minus, imag_plus, imag_minus])
    near_other = lax.ppermute(near, "core", CORE_PAIRS)
    far = jnp.stack([real_far, imag_far])
    far_other = lax.ppermute(far, "core", CORE_PAIRS)
    pieces = []
    for part in range(2):
        for src_first, src_near, src_far in ((first, near, far), (first_other, near_other, far_other)):
            pieces.extend([src_first[part], src_near[2 * part], src_far[part], src_near[2 * part + 1]])
    left = jnp.stack(pieces).reshape(2 * pairs, local_g)

    all_bands = column[:, :, width].astype(jnp.int32)
    gap = lookup(all_bands[1], conduction_energy) - lookup(all_bands[0], valence_energy)
    wide = column[:, :, :width].astype(jnp.float32)
    here = (lax.axis_index("x"), lax.axis_index("y"), lax.axis_index("core"))

    def relative(scaled, order):
        grid = scaled.reshape(nx, ny, ncore, local_pairs, width)
        for axis, start in enumerate(here):
            size = grid.shape[axis]
            doubled = jnp.concatenate([grid, grid], axis=axis)
            grid = lax.dynamic_slice_in_dim(doubled, start, size, axis=axis)
        return grid.transpose(order + (3, 4)).reshape(pairs, width)

    real_order = (2, 1, 0)
    imag_order = (2, 0, 1)
    right_real = []
    right_imag = []
    for index in range(frequency.shape[0]):
        omega = frequency[index]
        weight = 4.0 * gap / (gap * gap + omega * omega)
        scaled_real = (weight[:, None] * wide[0]).astype(jnp.bfloat16)
        scaled_imag = (weight[:, None] * wide[1]).astype(jnp.bfloat16)
        real_a = relative(scaled_real, real_order)
        imag_b = relative(scaled_imag, imag_order)
        real_b = relative(scaled_real, imag_order)
        imag_a = relative(scaled_imag, real_order)
        right_real.append(jnp.concatenate([-real_a, -imag_b], axis=0))
        right_imag.append(jnp.concatenate([-imag_a, real_b], axis=0))
    dims = (((0,), (0,)), ((), ()))
    chi_real = lax.dot_general(left, jnp.stack(right_real, axis=1), dims, preferred_element_type=jnp.float32)
    chi_imag = lax.dot_general(left, jnp.stack(right_imag, axis=1), dims, preferred_element_type=jnp.float32)
    chi_real = chi_real.transpose(1, 0, 2)
    chi_imag = chi_imag.transpose(1, 0, 2)
    return chi_real.astype(jnp.bfloat16), chi_imag.astype(jnp.bfloat16)


def solution(mesh):
    rows, cols = mesh.devices.shape
    grid = Mesh(mesh.devices.reshape(rows, 4, cols // 8, 2), ("row", "x", "y", "core"))
    cols = ("x", "y", "core")
    placed = (P(cols, "row"), P(cols, "row"), P(cols), P(cols), P(), P(), P())
    return jax.shard_map(
        on_device,
        mesh=grid,
        in_specs=placed,
        out_specs=(P(None, "row", cols), P(None, "row", cols)),
        check_vma=False,
    )
```

```python
import jax
import jax.numpy as jnp
from jax import lax
from jax.sharding import Mesh, PartitionSpec as P

CORE_PAIRS = [(0, 1), (1, 0)]


def lookup(indices, table):
    count = table.shape[0]
    picks = indices[:, None] == lax.broadcasted_iota(jnp.int32, (1, count), 1)
    return jnp.sum(jnp.where(picks, table[None, :], 0.0), axis=1)


def shift(value, axis, step):
    size = lax.psum(1, axis)
    return lax.ppermute(value, axis, [(i, (i + step) % size) for i in range(size)])


def ring_gather(block, axis):
    half = block.shape[-1] // 2
    from_minus = shift(block, axis, 1)
    from_plus = shift(block, axis, -1)
    far_first = shift(from_minus[..., :half], axis, 1)
    far_second = shift(from_plus[..., half:], axis, -1)
    far = jnp.concatenate([far_first, far_second], axis=-1)
    return from_plus, far, from_minus


def ring_direct(block, axis):
    return jnp.stack([block, shift(block, axis, -1), shift(block, axis, 2), shift(block, axis, 1)])


def on_device(
    matrix_real,
    matrix_imag,
    valence_index,
    conduction_index,
    valence_energy,
    conduction_energy,
    frequency,
):
    cols = ("x", "y", "core")
    nrow = lax.psum(1, "row")
    nx, ny, ncore = lax.psum(1, "x"), lax.psum(1, "y"), lax.psum(1, "core")
    ncol = nx * ny * ncore
    local_pairs, local_g = matrix_real.shape
    pairs = local_pairs * ncol
    width = local_g * nrow // ncol
    both = jnp.stack([matrix_real, matrix_imag])

    copies = jnp.broadcast_to(both[None], (nrow,) + both.shape)
    spread = lax.all_to_all(copies, "row", 0, 0, tiled=True)
    spread = spread.reshape(nrow, 2, local_pairs, local_g // width, width)
    row_real = ring_direct(matrix_real, "x")
    col_imag = ring_direct(matrix_imag, "y")
    first = jnp.stack([row_real, col_imag])
    first_other = lax.ppermute(first, "core", CORE_PAIRS)
    spread, col_imag = lax.optimization_barrier((spread, col_imag))
    payload = spread.transpose(0, 3, 1, 2, 4).reshape(ncol, 2, local_pairs, width)
    bands = jnp.stack([valence_index, conduction_index]).astype(jnp.bfloat16)
    tags = jnp.broadcast_to(bands[None, :, :, None], (ncol, 2, local_pairs, 128))
    payload = jnp.concatenate([payload, tags], axis=3)
    column = lax.all_to_all(payload, cols, split_axis=0, concat_axis=0, tiled=True)
    column = column.transpose(1, 0, 2, 3).reshape(2, pairs, width + 128)
    real_plus, real_far, real_minus = ring_gather(row_real, "y")
    imag_plus, imag_far, imag_minus = ring_gather(col_imag, "x")
    near = jnp.stack([real_plus, real_minus, imag_plus, imag_minus])
    near_other = lax.ppermute(near, "core", CORE_PAIRS)
    far = jnp.stack([real_far, imag_far])
    far_other = lax.ppermute(far, "core", CORE_PAIRS)
    parts = []
    for part in range(2):
        for src_first, src_near, src_far in ((first, near, far), (first_other, near_other, far_other)):
            parts.append(
                jnp.stack([src_first[part], src_near[2 * part], src_far[part], src_near[2 * part + 1]])
            )
    left = jnp.stack(parts).reshape(2 * pairs, local_g)

    all_bands = column[:, :, width].astype(jnp.int32)
    gap = lookup(all_bands[1], conduction_energy) - lookup(all_bands[0], valence_energy)
    wide = column[:, :, :width].astype(jnp.float32)
    here = (lax.axis_index("x"), lax.axis_index("y"), lax.axis_index("core"))

    def relative(scaled, order):
        grid = scaled.reshape(nx, ny, ncore, local_pairs, width)
        for axis, start in enumerate(here):
            size = grid.shape[axis]
            doubled = jnp.concatenate([grid, grid], axis=axis)
            grid = lax.dynamic_slice_in_dim(doubled, start, size, axis=axis)
        return grid.transpose(order + (3, 4)).reshape(pairs, width)

    real_order = (2, 1, 0)
    imag_order = (2, 0, 1)
    right_real = []
    right_imag = []
    for index in range(frequency.shape[0]):
        omega = frequency[index]
        weight = 4.0 * gap / (gap * gap + omega * omega)
        scaled_real = (weight[:, None] * wide[0]).astype(jnp.bfloat16)
        scaled_imag = (weight[:, None] * wide[1]).astype(jnp.bfloat16)
        real_a = relative(scaled_real, real_order)
        imag_b = relative(scaled_imag, imag_order)
        real_b = relative(scaled_real, imag_order)
        imag_a = relative(scaled_imag, real_order)
        right_real.append(jnp.concatenate([-real_a, -imag_b], axis=0))
        right_imag.append(jnp.concatenate([-imag_a, real_b], axis=0))
    dims = (((0,), (0,)), ((), ()))
    chi_real = lax.dot_general(left, jnp.stack(right_real, axis=1), dims, preferred_element_type=jnp.float32)
    chi_imag = lax.dot_general(left, jnp.stack(right_imag, axis=1), dims, preferred_element_type=jnp.float32)
    chi_real = chi_real.transpose(1, 0, 2)
    chi_imag = chi_imag.transpose(1, 0, 2)
    return chi_real.astype(jnp.bfloat16), chi_imag.astype(jnp.bfloat16)


def solution(mesh):
    rows, cols = mesh.devices.shape
    grid = Mesh(mesh.devices.reshape(rows, 4, cols // 8, 2), ("row", "x", "y", "core"))
    cols = ("x", "y", "core")
    placed = (P(cols, "row"), P(cols, "row"), P(cols), P(cols), P(), P(), P())
    return jax.shard_map(
        on_device,
        mesh=grid,
        in_specs=placed,
        out_specs=(P(None, "row", cols), P(None, "row", cols)),
        check_vma=False,
    )
```

```python
import jax
import jax.numpy as jnp
from jax import lax
from jax.sharding import Mesh, PartitionSpec as P

CORE_PAIRS = [(0, 1), (1, 0)]


def lookup(indices, table):
    count = table.shape[0]
    picks = indices[:, None] == lax.broadcasted_iota(jnp.int32, (1, count), 1)
    return jnp.sum(jnp.where(picks, table[None, :], 0.0), axis=1)


def shift(value, axis, step):
    size = lax.psum(1, axis)
    return lax.ppermute(value, axis, [(i, (i + step) % size) for i in range(size)])


def ring_gather(block, axis):
    half = block.shape[-1] // 2
    from_minus = shift(block, axis, 1)
    from_plus = shift(block, axis, -1)
    far_first = shift(from_minus[..., :half], axis, 1)
    far_second = shift(from_plus[..., half:], axis, -1)
    far = jnp.concatenate([far_first, far_second], axis=-1)
    return from_plus, far, from_minus


def ring_direct(block, axis):
    return jnp.stack([block, shift(block, axis, -1), shift(block, axis, 2), shift(block, axis, 1)])


def on_device(
    matrix_real,
    matrix_imag,
    valence_index,
    conduction_index,
    valence_energy,
    conduction_energy,
    frequency,
):
    cols = ("x", "y", "core")
    nrow = lax.psum(1, "row")
    nx, ny, ncore = lax.psum(1, "x"), lax.psum(1, "y"), lax.psum(1, "core")
    ncol = nx * ny * ncore
    local_pairs, local_g = matrix_real.shape
    pairs = local_pairs * ncol
    width = local_g * nrow // ncol
    both = jnp.stack([matrix_real, matrix_imag])

    copies = jnp.broadcast_to(both[None], (nrow,) + both.shape)
    spread = lax.all_to_all(copies, "row", 0, 0, tiled=True)
    spread = spread.reshape(nrow, 2, local_pairs, local_g // width, width)
    row_real = ring_direct(matrix_real, "x")
    col_imag = ring_direct(matrix_imag, "y")
    first = jnp.stack([row_real, col_imag])
    first_other = lax.ppermute(first, "core", CORE_PAIRS)
    spread, row_real, col_imag, first = lax.optimization_barrier((spread, row_real, col_imag, first))
    payload = spread.transpose(0, 3, 1, 2, 4).reshape(ncol, 2, local_pairs, width)
    bands = jnp.stack([valence_index, conduction_index]).astype(jnp.bfloat16)
    tags = jnp.broadcast_to(bands[None, :, :, None], (ncol, 2, local_pairs, 128))
    payload = jnp.concatenate([payload, tags], axis=3)
    column = lax.all_to_all(payload, cols, split_axis=0, concat_axis=0, tiled=True)
    column = column.transpose(1, 0, 2, 3).reshape(2, pairs, width + 128)
    real_plus, real_far, real_minus = ring_gather(row_real, "y")
    imag_plus, imag_far, imag_minus = ring_gather(col_imag, "x")
    near = jnp.stack([real_plus, real_minus, imag_plus, imag_minus])
    far = jnp.stack([real_far, imag_far])
    near, far = lax.optimization_barrier((near, far))
    near_other = lax.ppermute(near, "core", CORE_PAIRS)
    far_other = lax.ppermute(far, "core", CORE_PAIRS)
    parts = []
    for part in range(2):
        for src_first, src_near, src_far in ((first, near, far), (first_other, near_other, far_other)):
            parts.append(
                jnp.stack([src_first[part], src_near[2 * part], src_far[part], src_near[2 * part + 1]])
            )
    left = jnp.stack(parts).reshape(2 * pairs, local_g)

    all_bands = column[:, :, width].astype(jnp.int32)
    gap = lookup(all_bands[1], conduction_energy) - lookup(all_bands[0], valence_energy)
    wide = column[:, :, :width].astype(jnp.float32)
    here = (lax.axis_index("x"), lax.axis_index("y"), lax.axis_index("core"))

    def relative(scaled, order):
        grid = scaled.reshape(nx, ny, ncore, local_pairs, width)
        for axis, start in enumerate(here):
            size = grid.shape[axis]
            doubled = jnp.concatenate([grid, grid], axis=axis)
            grid = lax.dynamic_slice_in_dim(doubled, start, size, axis=axis)
        return grid.transpose(order + (3, 4)).reshape(pairs, width)

    real_order = (2, 1, 0)
    imag_order = (2, 0, 1)
    right_real = []
    right_imag = []
    for index in range(frequency.shape[0]):
        omega = frequency[index]
        weight = 4.0 * gap / (gap * gap + omega * omega)
        scaled_real = (weight[:, None] * wide[0]).astype(jnp.bfloat16)
        scaled_imag = (weight[:, None] * wide[1]).astype(jnp.bfloat16)
        real_a = relative(scaled_real, real_order)
        imag_b = relative(scaled_imag, imag_order)
        real_b = relative(scaled_real, imag_order)
        imag_a = relative(scaled_imag, real_order)
        right_real.append(jnp.concatenate([-real_a, -imag_b], axis=0))
        right_imag.append(jnp.concatenate([-imag_a, real_b], axis=0))
    dims = (((0,), (0,)), ((), ()))
    chi_real = lax.dot_general(left, jnp.stack(right_real, axis=1), dims, preferred_element_type=jnp.float32)
    chi_imag = lax.dot_general(left, jnp.stack(right_imag, axis=1), dims, preferred_element_type=jnp.float32)
    chi_real = chi_real.transpose(1, 0, 2)
    chi_imag = chi_imag.transpose(1, 0, 2)
    return chi_real.astype(jnp.bfloat16), chi_imag.astype(jnp.bfloat16)


def solution(mesh):
    rows, cols = mesh.devices.shape
    grid = Mesh(mesh.devices.reshape(rows, 4, cols // 8, 2), ("row", "x", "y", "core"))
    cols = ("x", "y", "core")
    placed = (P(cols, "row"), P(cols, "row"), P(cols), P(cols), P(), P(), P())
    return jax.shard_map(
        on_device,
        mesh=grid,
        in_specs=placed,
        out_specs=(P(None, "row", cols), P(None, "row", cols)),
        check_vma=False,
    )
```

```python
import jax
import jax.numpy as jnp
from jax import lax
from jax.sharding import Mesh, PartitionSpec as P

CORE_PAIRS = [(0, 1), (1, 0)]


def lookup(indices, table):
    count = table.shape[0]
    picks = indices[:, None] == lax.broadcasted_iota(jnp.int32, (1, count), 1)
    return jnp.sum(jnp.where(picks, table[None, :], 0.0), axis=1)


def shift(value, axis, step):
    size = lax.psum(1, axis)
    return lax.ppermute(value, axis, [(i, (i + step) % size) for i in range(size)])


def ring_gather(block, axis):
    half = block.shape[-1] // 2
    from_minus = shift(block, axis, 1)
    from_plus = shift(block, axis, -1)
    far_first = shift(from_minus[..., :half], axis, 1)
    far_second = shift(from_plus[..., half:], axis, -1)
    return from_plus, (far_first, far_second), from_minus


def ring_direct(block, axis):
    return jnp.stack([block, shift(block, axis, -1), shift(block, axis, 2), shift(block, axis, 1)])


def on_device(
    matrix_real,
    matrix_imag,
    valence_index,
    conduction_index,
    valence_energy,
    conduction_energy,
    frequency,
):
    cols = ("x", "y", "core")
    nrow = lax.psum(1, "row")
    nx, ny, ncore = lax.psum(1, "x"), lax.psum(1, "y"), lax.psum(1, "core")
    ncol = nx * ny * ncore
    local_pairs, local_g = matrix_real.shape
    pairs = local_pairs * ncol
    width = local_g * nrow // ncol
    both = jnp.stack([matrix_real, matrix_imag])

    copies = jnp.broadcast_to(both[None], (nrow,) + both.shape)
    spread = lax.all_to_all(copies, "row", 0, 0, tiled=True)
    spread = spread.reshape(nrow, 2, local_pairs, local_g // width, width)
    row_real = ring_direct(matrix_real, "x")
    col_imag = ring_direct(matrix_imag, "y")
    first = jnp.stack([row_real, col_imag])
    first_other = lax.ppermute(first, "core", CORE_PAIRS)
    spread, row_real, col_imag, first = lax.optimization_barrier((spread, row_real, col_imag, first))
    payload = spread.transpose(0, 3, 1, 2, 4).reshape(ncol, 2, local_pairs, width)
    bands = jnp.stack([valence_index, conduction_index]).astype(jnp.bfloat16)
    tags = jnp.broadcast_to(bands[None, :, :, None], (ncol, 2, local_pairs, 128))
    payload = jnp.concatenate([payload, tags], axis=3)
    column = lax.all_to_all(payload, cols, split_axis=0, concat_axis=0, tiled=True)
    column = column.transpose(1, 0, 2, 3).reshape(2, pairs, width + 128)
    real_plus, real_far, real_minus = ring_gather(row_real, "y")
    imag_plus, imag_far, imag_minus = ring_gather(col_imag, "x")
    near = jnp.stack([real_plus, real_minus, imag_plus, imag_minus])
    near_other = lax.ppermute(near, "core", CORE_PAIRS)
    far_a = jnp.stack([real_far[0], imag_far[0]])
    far_a_other = lax.ppermute(far_a, "core", CORE_PAIRS)
    far_b = jnp.stack([real_far[1], imag_far[1]])
    far_b_other = lax.ppermute(far_b, "core", CORE_PAIRS)
    far = jnp.concatenate([far_a, far_b], axis=-1)
    far_other = jnp.concatenate([far_a_other, far_b_other], axis=-1)
    parts = []
    for part in range(2):
        for src_first, src_near, src_far in ((first, near, far), (first_other, near_other, far_other)):
            parts.append(
                jnp.stack([src_first[part], src_near[2 * part], src_far[part], src_near[2 * part + 1]])
            )
    left = jnp.stack(parts).reshape(2 * pairs, local_g)

    all_bands = column[:, :, width].astype(jnp.int32)
    gap = lookup(all_bands[1], conduction_energy) - lookup(all_bands[0], valence_energy)
    wide = column[:, :, :width].astype(jnp.float32)
    here = (lax.axis_index("x"), lax.axis_index("y"), lax.axis_index("core"))

    def relative(scaled, order):
        grid = scaled.reshape(nx, ny, ncore, local_pairs, width)
        for axis, start in enumerate(here):
            size = grid.shape[axis]
            doubled = jnp.concatenate([grid, grid], axis=axis)
            grid = lax.dynamic_slice_in_dim(doubled, start, size, axis=axis)
        return grid.transpose(order + (3, 4)).reshape(pairs, width)

    real_order = (2, 1, 0)
    imag_order = (2, 0, 1)
    right_real = []
    right_imag = []
    for index in range(frequency.shape[0]):
        omega = frequency[index]
        weight = 4.0 * gap / (gap * gap + omega * omega)
        scaled_real = (weight[:, None] * wide[0]).astype(jnp.bfloat16)
        scaled_imag = (weight[:, None] * wide[1]).astype(jnp.bfloat16)
        real_a = relative(scaled_real, real_order)
        imag_b = relative(scaled_imag, imag_order)
        real_b = relative(scaled_real, imag_order)
        imag_a = relative(scaled_imag, real_order)
        right_real.append(jnp.concatenate([-real_a, -imag_b], axis=0))
        right_imag.append(jnp.concatenate([-imag_a, real_b], axis=0))
    dims = (((0,), (0,)), ((), ()))
    chi_real = lax.dot_general(left, jnp.stack(right_real, axis=1), dims, preferred_element_type=jnp.float32)
    chi_imag = lax.dot_general(left, jnp.stack(right_imag, axis=1), dims, preferred_element_type=jnp.float32)
    chi_real = chi_real.transpose(1, 0, 2)
    chi_imag = chi_imag.transpose(1, 0, 2)
    return chi_real.astype(jnp.bfloat16), chi_imag.astype(jnp.bfloat16)


def solution(mesh):
    rows, cols = mesh.devices.shape
    grid = Mesh(mesh.devices.reshape(rows, 4, cols // 8, 2), ("row", "x", "y", "core"))
    cols = ("x", "y", "core")
    placed = (P(cols, "row"), P(cols, "row"), P(cols), P(cols), P(), P(), P())
    return jax.shard_map(
        on_device,
        mesh=grid,
        in_specs=placed,
        out_specs=(P(None, "row", cols), P(None, "row", cols)),
        check_vma=False,
    )
```
